768 devices in a mesh: lat: 16 (over x_hi, y), lon: 24 (over z, core), pipe: 2 (over x_lo).
Axes of the slice: x: 4 (x_hi: 2, x_lo: 2; x = x_hi * 2 + x_lo), y: 8, z: 12, core: 2. Of those that a mesh axis runs over, the one named last changes fastest.
Arguments:
- queries_keys: bfloat16 [2, 2, 256, 192, 1536], P('pipe', None, 'lat', 'lon'), may hold values from -30 to 30
- values: bfloat16 [2, 256, 192, 1536], P('pipe', 'lat', 'lon'), may hold values from -6 to 6
- cotangent: bfloat16 [256, 192, 1536], P('lat', 'lon'), may hold values from -6 to 6
Outputs:
- activations: bfloat16 [2, 256, 192, 1536], P('pipe', 'lat', 'lon')
- grad_queries_keys: bfloat16 [2, 2, 256, 192, 1536], P('pipe', None, 'lat', 'lon')
- grad_values: bfloat16 [2, 256, 192, 1536], P('pipe', 'lat', 'lon')
The draws below stay inside these ranges and needn't reach their ends.
All inputs are finite; a program needn't handle non-finite values.
Results may differ from the reference program's by a relative error of at most 0.0063.
Values may be sent and summed in bfloat16 or wider, within the bound.
No kernel may reach another device: no remote copies, remote signals or barrier semaphores. Data moves between devices by JAX's collectives and lax.ppermute only.
A program may use at most 64 MiB of HBM per device.

```python
import math
import jax
import jax.numpy as jnp
from jax import lax

HEADS = 12
TL = 16
TN = 8
MARGIN = 2
HD = 1536
NLAT = 256
NLON = 192
SECTIONS = 2


def draw_queries_keys(key, part):
    streams = jax.random.split(jax.random.fold_in(key, 17), 2)
    shape = (SECTIONS, NLAT, NLON, HD)
    queries = 2.5 * jnp.clip(jax.random.normal(streams[0], shape, jnp.float32), -4.0, 4.0)
    drawn = jnp.clip(jax.random.normal(streams[1], shape, jnp.float32), -5.0, 5.0)
    return jnp.stack([queries, drawn], axis=1).astype(jnp.bfloat16)


def block_levels(stream_key, dims, cuts, least, top_value):
    gain, own = 1.0, jax.random.fold_in(stream_key, 6)
    for dim, blocks in cuts:
        draws = jnp.exp(jax.random.uniform(jax.random.fold_in(own, dim), (blocks,), jnp.float32, least / len(cuts), top_value / len(cuts)))
        gain = gain * jnp.repeat(draws, dims[dim] // blocks).reshape([-1 if axis == dim else 1 for axis in range(len(dims))])
    return gain


def scatter_about(stream_key, shape, spread, most, shards=(), held_as=jnp.bfloat16):
    values = jax.random.normal(stream_key, shape, jnp.float32) * spread
    if len(shards) > 0:
        values = block_levels(stream_key, shape, shards, -0.22, 0.18) * values
    return jnp.clip(values, min=-most, max=most).astype(held_as)


def setup_inputs(seed: int = 0) -> dict:
    streams_of = jax.random.split(jax.random.key(seed), 4)
    queries_keys = draw_queries_keys(jax.random.fold_in(streams_of[3], 71), 0)
    values = scatter_about(streams_of[1], (SECTIONS, NLAT, NLON, HD), 1.0, 6.0, ((0, 2), (1, 16), (2, 24)))
    cotangent = scatter_about(streams_of[2], (NLAT, NLON, HD), 1.0, 6.0, ((0, 16), (1, 24)))
    return dict(queries_keys=queries_keys, values=values, cotangent=cotangent)


NEGATIVE = -1e+30

def softmax_rows(query_head, key_head, allowed, scaling):
    scores = jnp.dot(query_head, key_head.T, preferred_element_type=jnp.float32) * scaling
    scores = jnp.where(allowed[None, :], scores, NEGATIVE)
    highest = lax.optimization_barrier(jnp.max(scores, axis=1, keepdims=True))
    weights = jnp.exp(scores - highest)
    return weights / lax.optimization_barrier(jnp.sum(weights, axis=1, keepdims=True))

def head_forward(query_head, key_head, value_head, allowed, scaling):
    weights = softmax_rows(query_head, key_head, allowed, scaling)
    return jnp.dot(weights.astype(jnp.bfloat16), value_head, preferred_element_type=jnp.float32).astype(jnp.bfloat16)

def head_backward(query_head, key_head, value_head, upstream_head, allowed, scaling):
    weights = softmax_rows(query_head, key_head, allowed, scaling)
    weights_low = weights.astype(jnp.bfloat16)
    dweights = jnp.dot(upstream_head, value_head.T, preferred_element_type=jnp.float32)
    inner = lax.optimization_barrier(jnp.sum(weights * dweights, axis=1, keepdims=True))
    dscore = (weights * (dweights - inner) * scaling).astype(jnp.bfloat16)
    grad_query = jnp.dot(dscore, key_head, preferred_element_type=jnp.float32).astype(jnp.bfloat16)
    grad_key = jnp.dot(dscore.T, query_head, preferred_element_type=jnp.float32)
    grad_value = jnp.dot(weights_low.T, upstream_head, preferred_element_type=jnp.float32)
    return (grad_query, grad_key, grad_value)

def split_heads(field, heads):
    return field.reshape(field.shape[0], heads, -1).transpose(1, 0, 2)

def join_heads(field):
    return field.transpose(1, 0, 2).reshape(field.shape[1], -1)

def tile_forward(queries, keys_ext, values_ext, allowed, heads):
    scaling = 1.0 / math.sqrt(queries.shape[1] // heads)

    def one_head(operands):
        return head_forward(operands[0], operands[1], operands[2], allowed, scaling)
    result = lax.map(one_head, (split_heads(queries, heads), split_heads(keys_ext, heads), split_heads(values_ext, heads)))
    return join_heads(result)

def tile_backward(queries, keys_ext, values_ext, upstream, allowed, heads):
    scaling = 1.0 / math.sqrt(queries.shape[1] // heads)

    def one_head(operands):
        return head_backward(operands[0], operands[1], operands[2], operands[3], allowed, scaling)
    result = lax.map(one_head, (split_heads(queries, heads), split_heads(keys_ext, heads), split_heads(values_ext, heads), split_heads(upstream, heads)))
    return (join_heads(result[0]), join_heads(result[1]), join_heads(result[2]))

def reference(queries_keys, values, cotangent):
    section_count = queries_keys.shape[0]
    lat_total, lon_total, features = cotangent.shape
    tile_rows = TL
    tile_cols = TN
    margin = MARGIN
    rows_ext = tile_rows + 2 * margin
    cols_ext = tile_cols + 2 * margin
    tiles_lat = lat_total // tile_rows
    tiles_lon = lon_total // tile_cols
    tile_count = tiles_lat * tiles_lon
    zero = jnp.zeros((), jnp.int32)

    def window_allowed(tile_lat):
        lat_rows = tile_lat * tile_rows - margin + jnp.arange(rows_ext, dtype=jnp.int32)
        inside = (lat_rows >= 0) & (lat_rows < lat_total)
        return jnp.broadcast_to(inside[:, None], (rows_ext, cols_ext)).reshape(-1)

    def wrap_pad(field):
        field = jnp.concatenate([field[lat_total - margin:], field, field[:margin]], axis=0)
        return jnp.concatenate([field[:, lon_total - margin:], field, field[:, :margin]], axis=1)

    def tile_slices(index, query_field, key_pad, value_pad):
        tile_lat = index // tiles_lon
        tile_lon = index % tiles_lon
        row_start = (tile_lat * tile_rows).astype(jnp.int32)
        col_start = (tile_lon * tile_cols).astype(jnp.int32)
        query_tile = lax.dynamic_slice(query_field, (row_start, col_start, zero), (tile_rows, tile_cols, features)).reshape(-1, features)
        key_tile = lax.dynamic_slice(key_pad, (row_start, col_start, zero), (rows_ext, cols_ext, features)).reshape(-1, features)
        value_tile = lax.dynamic_slice(value_pad, (row_start, col_start, zero), (rows_ext, cols_ext, features)).reshape(-1, features)
        return (tile_lat, row_start, col_start, query_tile, key_tile, value_tile)

    def assemble(blocks):
        blocks = blocks.reshape(tiles_lat, tiles_lon, tile_rows, tile_cols, features)
        return blocks.transpose(0, 2, 1, 3, 4).reshape(lat_total, lon_total, features)

    def section_forward(query_field, key_field, value_field):
        key_pad = wrap_pad(key_field)
        value_pad = wrap_pad(value_field)

        def one_tile(index):
            tile_lat, row_start, col_start, query_tile, key_tile, value_tile = tile_slices(index, query_field, key_pad, value_pad)
            result = tile_forward(query_tile, key_tile, value_tile, window_allowed(tile_lat), HEADS)
            return result.reshape(tile_rows, tile_cols, features)
        return assemble(lax.map(one_tile, jnp.arange(tile_count, dtype=jnp.int32)))
    row_ids = jnp.arange(rows_ext, dtype=jnp.int32)[:, None]
    col_ids = jnp.arange(cols_ext, dtype=jnp.int32)[None, :]
    centre = (row_ids >= margin) & (row_ids < margin + tile_rows) & (col_ids >= margin) & (col_ids < margin + tile_cols)

    def section_backward(query_field, key_field, value_field, upstream_field):
        key_pad = wrap_pad(key_field)
        value_pad = wrap_pad(value_field)

        def one_tile(total, index):
            tile_lat, row_start, col_start, query_tile, key_tile, value_tile = tile_slices(index, query_field, key_pad, value_pad)
            upstream_tile = lax.dynamic_slice(upstream_field, (row_start, col_start, zero), (tile_rows, tile_cols, features)).reshape(-1, features)
            grad_query, grad_key, grad_value = tile_backward(query_tile, key_tile, value_tile, upstream_tile, window_allowed(tile_lat), HEADS)
            ext = jnp.stack([grad_key.reshape(rows_ext, cols_ext, features), grad_value.reshape(rows_ext, cols_ext, features)], axis=2)
            rounded = lax.optimization_barrier(ext.astype(jnp.bfloat16)).astype(jnp.float32)
            term = jnp.where(centre[:, :, None, None], ext, rounded)
            start = (row_start, col_start, zero, zero)
            total = lax.dynamic_update_slice(total, lax.dynamic_slice(total, start, ext.shape) + term, start)
            return (total, grad_query.reshape(tile_rows, tile_cols, features))
        initial = jnp.zeros((lat_total + 2 * margin, lon_total + 2 * margin, 2, features), jnp.float32)
        total, blocks = lax.scan(one_tile, initial, jnp.arange(tile_count, dtype=jnp.int32))
        core = total[margin:margin + lat_total]
        core = core.at[:margin].add(total[margin + lat_total:])
        core = core.at[lat_total - margin:].add(total[:margin])
        folded = core[:, margin:margin + lon_total]
        folded = folded.at[:, :margin].add(core[:, margin + lon_total:])
        folded = folded.at[:, lon_total - margin:].add(core[:, :margin])
        folded = folded.astype(jnp.bfloat16)
        return (assemble(blocks), folded[:, :, 0], folded[:, :, 1])
    previous = jnp.zeros((lat_total, lon_total, features), jnp.float32)
    section_inputs = []
    contexts = []
    for level in range(section_count):
        inputs = (values[level].astype(jnp.float32) + previous).astype(jnp.bfloat16)
        context = section_forward(queries_keys[level, 0], queries_keys[level, 1], inputs)
        section_inputs.append(inputs)
        contexts.append(context)
        previous = context.astype(jnp.float32)
    upstream = cotangent
    grads_pair = [None] * section_count
    grads_value = [None] * section_count
    for level in reversed(range(section_count)):
        grad_query, grad_key, grad_value = section_backward(queries_keys[level, 0], queries_keys[level, 1], section_inputs[level], upstream)
        grads_pair[level] = jnp.stack([grad_query, grad_key], axis=0)
        grads_value[level] = grad_value
        upstream = grad_value
    return (jnp.stack(contexts, axis=0), jnp.stack(grads_pair, axis=0), jnp.stack(grads_value, axis=0))
```

```python
import math

import jax
import jax.numpy as jnp
from jax import lax
from jax.sharding import PartitionSpec as P

HEADS = 12
MARGIN = 2

NEGATIVE = -1e30

AXES = ("lat", "lon", "pipe")
NEIGHBOURS = [(dl, dn) for dl in (-1, 0, 1) for dn in (-1, 0, 1) if (dl, dn) != (0, 0)]


def linear(l, n, p, lons, pipes):
    return (l * lons + n) * pipes + p


def pairs_from(offset, sizes, src_pipe=None, dst_pipe=None):
    lats, lons, pipes = sizes
    dl, dn = offset
    out = []
    for l in range(lats):
        sl = l + dl
        if sl < 0 or sl >= lats:
            continue
        for n in range(lons):
            sn = (n + dn) % lons
            if src_pipe is None:
                for p in range(pipes):
                    out.append((linear(sl, sn, p, lons, pipes), linear(l, n, p, lons, pipes)))
            else:
                out.append((linear(sl, sn, src_pipe, lons, pipes), linear(l, n, dst_pipe, lons, pipes)))
    return out


def edge(length, d):
    if d == -1:
        return slice(length - MARGIN, length)
    if d == 1:
        return slice(0, MARGIN)
    return slice(0, length)


def gather_window(tile, sizes, src_pipe=None, dst_pipe=None):
    rows, cols = tile.shape[0], tile.shape[1]
    pieces = {}
    for off in [(0, 0)] + NEIGHBOURS:
        dl, dn = off
        if off == (0, 0) and src_pipe is None:
            pieces[off] = tile
            continue
        part = tile[edge(rows, dl), edge(cols, dn)]
        pieces[off] = lax.ppermute(part, AXES, pairs_from(off, sizes, src_pipe, dst_pipe))
    bands = []
    for dl in (-1, 0, 1):
        bands.append(jnp.concatenate([pieces[(dl, dn)] for dn in (-1, 0, 1)], axis=1))
    return jnp.concatenate(bands, axis=0)


def window_part(length, d):
    if d == -1:
        return slice(length + MARGIN, length + 2 * MARGIN)
    if d == 1:
        return slice(0, MARGIN)
    return slice(MARGIN, length + MARGIN)


def scatter_pieces(window, sizes, src_pipe=None, dst_pipe=None):
    rows, cols = window.shape[0] - 2 * MARGIN, window.shape[1] - 2 * MARGIN
    got = {}
    for off in NEIGHBOURS:
        dl, dn = off
        part = window[window_part(rows, dl), window_part(cols, dn)].astype(jnp.bfloat16)
        got[off] = lax.ppermute(part, AXES, pairs_from(off, sizes, src_pipe, dst_pipe))
    return got


def sum_pieces(centre, got):
    rows, cols = centre.shape[0], centre.shape[1]
    total = centre
    for (dl, dn), piece in got.items():
        piece = piece.astype(jnp.float32)
        r0 = 0 if dl <= 0 else rows - MARGIN
        c0 = 0 if dn <= 0 else cols - MARGIN
        pr = [(r0, rows - r0 - piece.shape[0])]
        pc = [(c0, cols - c0 - piece.shape[1])]
        pad = pr + pc + [(0, 0)] * (piece.ndim - 2)
        total = total + jnp.pad(piece, pad)
    return total


def probabilities(q3, k3, allowed, scaling):
    scores = jnp.einsum("thd,phd->htp", q3, k3, preferred_element_type=jnp.float32) * scaling
    scores = jnp.where(allowed[None, None, :], scores, NEGATIVE)
    highest = jnp.max(scores, axis=2, keepdims=True)
    weights = jnp.exp(scores - highest)
    return weights / jnp.sum(weights, axis=2, keepdims=True)


def attend(probs_low, u3):
    return jnp.einsum("htp,phd->thd", probs_low, u3, preferred_element_type=jnp.float32).astype(
        jnp.bfloat16
    )


def backward(probs, probs_low, q3, k3, u3, d3, scaling):
    dprob = jnp.einsum("thd,phd->htp", d3, u3, preferred_element_type=jnp.float32)
    inner = jnp.sum(probs * dprob, axis=2, keepdims=True)
    dscore = (probs * (dprob - inner) * scaling).astype(jnp.bfloat16)
    grad_q = jnp.einsum("htp,phd->thd", dscore, k3, preferred_element_type=jnp.float32).astype(
        jnp.bfloat16
    )
    kterm = jnp.einsum("htp,thd->phd", dscore, q3, preferred_element_type=jnp.float32)
    vterm = jnp.einsum("htp,thd->phd", probs_low, d3, preferred_element_type=jnp.float32)
    return grad_q, kterm, vterm


def body(queries_keys, values, cotangent):
    sizes = (lax.axis_size("lat"), lax.axis_size("lon"), lax.axis_size("pipe"))
    is_first = lax.axis_index("pipe") == 0
    tile_rows, tile_cols, features = cotangent.shape
    margin = MARGIN
    rows_ext = tile_rows + 2 * margin
    cols_ext = tile_cols + 2 * margin
    window_size = rows_ext * cols_ext
    token_count = tile_rows * tile_cols
    head_dim = features // HEADS
    scaling = 1.0 / math.sqrt(head_dim)

    q3 = queries_keys[0, 0].reshape(token_count, HEADS, head_dim)
    lat_rows = lax.axis_index("lat") * tile_rows - margin + jnp.arange(rows_ext, dtype=jnp.int32)
    inside = (lat_rows >= 0) & (lat_rows < tile_rows * sizes[0])
    allowed = jnp.broadcast_to(inside[:, None], (rows_ext, cols_ext)).reshape(window_size)

    kv = gather_window(jnp.stack([queries_keys[0, 1], values[0]], axis=2), sizes)
    k3 = kv[:, :, 0].reshape(window_size, HEADS, head_dim)
    v_win = kv[:, :, 1]

    probs_a = probabilities(q3, k3, allowed, scaling)
    context_a = attend(probs_a.astype(jnp.bfloat16), v_win.reshape(window_size, HEADS, head_dim))
    context_a = context_a.reshape(tile_rows, tile_cols, features)

    c_win = gather_window(context_a, sizes, src_pipe=0, dst_pipe=1)
    u_win = (v_win.astype(jnp.float32) + c_win.astype(jnp.float32)).astype(jnp.bfloat16)
    u3 = u_win.reshape(window_size, HEADS, head_dim)

    probs_b = probabilities(q3, k3, allowed, scaling)
    probs_b_low = probs_b.astype(jnp.bfloat16)
    context_b = attend(probs_b_low, u3).reshape(tile_rows, tile_cols, features)
    d3_b = cotangent.reshape(token_count, HEADS, head_dim)
    gq_b, kterm_b, vterm_b = backward(probs_b, probs_b_low, q3, k3, u3, d3_b, scaling)
    vterm_b = vterm_b.reshape(rows_ext, cols_ext, features)
    kterm_b = kterm_b.reshape(rows_ext, cols_ext, features)

    centre = slice(margin, margin + tile_rows), slice(margin, margin + tile_cols)
    got = scatter_pieces(vterm_b, sizes, src_pipe=1, dst_pipe=0)
    own_b = lax.ppermute(vterm_b[centre], AXES, pairs_from((0, 0), sizes, 1, 0))
    d_c = sum_pieces(own_b, got).astype(jnp.bfloat16)

    d3_c = d_c.reshape(token_count, HEADS, head_dim)
    gq_c, kterm_c, vterm_c = backward(probs_b, probs_b_low, q3, k3, u3, d3_c, scaling)
    kterm_c = kterm_c.reshape(rows_ext, cols_ext, features)
    vterm_c = vterm_c.reshape(rows_ext, cols_ext, features)

    terms = jnp.where(
        is_first, jnp.stack([kterm_c, vterm_c], axis=2), jnp.stack([kterm_b, vterm_b], axis=2)
    )
    back = scatter_pieces(terms, sizes)
    owned = sum_pieces(terms[centre], back).astype(jnp.bfloat16)

    activations = jnp.where(is_first, context_a, context_b)
    grad_q = jnp.where(is_first, gq_c, gq_b).reshape(tile_rows, tile_cols, features)
    grad_qk = jnp.stack([grad_q, owned[:, :, 0]], axis=0)
    return activations[None], grad_qk[None], owned[:, :, 1][None]


def solution(mesh):
    in_specs = (
        P("pipe", None, "lat", "lon", None),
        P("pipe", "lat", "lon", None),
        P("lat", "lon", None),
    )
    out_specs = (
        P("pipe", "lat", "lon", None),
        P("pipe", None, "lat", "lon", None),
        P("pipe", "lat", "lon", None),
    )
    return jax.shard_map(body, mesh=mesh, in_specs=in_specs, out_specs=out_specs, check_vma=False)
```

```python
import functools
import math

import jax
import jax.numpy as jnp
from jax import lax
from jax.experimental import pallas as pl
from jax.experimental.pallas import tpu as pltpu
from jax.sharding import PartitionSpec as P

HEADS = 12
MARGIN = 2

NEGATIVE = -1e30

AXES = ("lat", "lon", "pipe")
NEIGHBOURS = [(dl, dn) for dl in (-1, 0, 1) for dn in (-1, 0, 1) if (dl, dn) != (0, 0)]


def linear(l, n, p, lons, pipes):
    return (l * lons + n) * pipes + p


def pairs_from(offset, sizes, src_pipe=None, dst_pipe=None):
    lats, lons, pipes = sizes
    dl, dn = offset
    out = []
    for l in range(lats):
        sl = l + dl
        if sl < 0 or sl >= lats:
            continue
        for n in range(lons):
            sn = (n + dn) % lons
            if src_pipe is None:
                for p in range(pipes):
                    out.append((linear(sl, sn, p, lons, pipes), linear(l, n, p, lons, pipes)))
            else:
                out.append((linear(sl, sn, src_pipe, lons, pipes), linear(l, n, dst_pipe, lons, pipes)))
    return out


def edge(length, d):
    if d == -1:
        return slice(length - MARGIN, length)
    if d == 1:
        return slice(0, MARGIN)
    return slice(0, length)


def gather_window(tile, sizes, src_pipe=None, dst_pipe=None):
    rows, cols = tile.shape[0], tile.shape[1]
    pieces = {}
    for off in [(0, 0)] + NEIGHBOURS:
        dl, dn = off
        if off == (0, 0) and src_pipe is None:
            pieces[off] = tile
            continue
        part = tile[edge(rows, dl), edge(cols, dn)]
        pieces[off] = lax.ppermute(part, AXES, pairs_from(off, sizes, src_pipe, dst_pipe))
    bands = []
    for dl in (-1, 0, 1):
        bands.append(jnp.concatenate([pieces[(dl, dn)] for dn in (-1, 0, 1)], axis=1))
    return jnp.concatenate(bands, axis=0)


def window_part(length, d):
    if d == -1:
        return slice(length + MARGIN, length + 2 * MARGIN)
    if d == 1:
        return slice(0, MARGIN)
    return slice(MARGIN, length + MARGIN)


def scatter_pieces(window, sizes, src_pipe=None, dst_pipe=None):
    rows, cols = window.shape[0] - 2 * MARGIN, window.shape[1] - 2 * MARGIN
    got = {}
    for off in NEIGHBOURS:
        dl, dn = off
        part = window[window_part(rows, dl), window_part(cols, dn)].astype(jnp.bfloat16)
        got[off] = lax.ppermute(part, AXES, pairs_from(off, sizes, src_pipe, dst_pipe))
    return got


def sum_pieces(centre, got):
    rows, cols = centre.shape[0], centre.shape[1]
    total = centre
    for (dl, dn), piece in got.items():
        piece = piece.astype(jnp.float32)
        r0 = 0 if dl <= 0 else rows - MARGIN
        c0 = 0 if dn <= 0 else cols - MARGIN
        pr = [(r0, rows - r0 - piece.shape[0])]
        pc = [(c0, cols - c0 - piece.shape[1])]
        pad = pr + pc + [(0, 0)] * (piece.ndim - 2)
        total = total + jnp.pad(piece, pad)
    return total


def attention_kernel(scaling, with_context, with_backward, *refs):
    mask_ref, q_ref, k_ref, u_ref = refs[:4]
    refs = refs[4:]
    if with_backward:
        d_ref, refs = refs[0], refs[1:]
    if with_context:
        c_ref, refs = refs[0], refs[1:]
    if with_backward:
        gq_ref, kt_ref, vt_ref = refs
    head_dim = q_ref.shape[1] // HEADS
    nt = (((1,), (1,)), ((), ()))

    def head(h, carry):
        lanes = pl.ds(pl.multiple_of(h * head_dim, head_dim), head_dim)
        qh = q_ref[:, lanes]
        kh = k_ref[:, lanes]
        uh = u_ref[:, lanes]
        scores = lax.dot_general(qh, kh, nt, preferred_element_type=jnp.float32) * scaling
        scores = jnp.where(mask_ref[...] > 0.5, scores, NEGATIVE)
        highest = jnp.max(scores, axis=1, keepdims=True)
        weights = jnp.exp(scores - highest)
        probs = weights / jnp.sum(weights, axis=1, keepdims=True)
        probs_low = probs.astype(jnp.bfloat16)
        if with_context:
            c_ref[:, lanes] = jnp.dot(
                probs_low, uh, preferred_element_type=jnp.float32
            ).astype(c_ref.dtype)
        if with_backward:
            dh = d_ref[:, lanes]
            dprob = lax.dot_general(dh, uh, nt, preferred_element_type=jnp.float32)
            inner = jnp.sum(probs * dprob, axis=1, keepdims=True)
            dscore = probs * (dprob - inner) * scaling
            gq_ref[:, lanes] = jnp.dot(
                dscore.astype(jnp.bfloat16), kh, preferred_element_type=jnp.float32
            ).astype(gq_ref.dtype)
            kt_ref[:, lanes] = jnp.dot(
                dscore.T.astype(jnp.bfloat16), qh, preferred_element_type=jnp.float32
            )
            vt_ref[:, lanes] = jnp.dot(
                probs.T.astype(jnp.bfloat16), dh, preferred_element_type=jnp.float32
            )
        return carry

    lax.fori_loop(0, HEADS, head, 0)


def attention(mask, q, k, u, d=None, with_context=True, scaling=1.0):
    tokens, features = q.shape
    keys = k.shape[0]
    with_backward = d is not None
    outs = []
    if with_context:
        outs.append(jax.ShapeDtypeStruct((tokens, features), jnp.bfloat16))
    if with_backward:
        outs += [
            jax.ShapeDtypeStruct((tokens, features), jnp.bfloat16),
            jax.ShapeDtypeStruct((keys, features), jnp.float32),
            jax.ShapeDtypeStruct((keys, features), jnp.float32),
        ]
    args = [mask, q, k, u] + ([d] if with_backward else [])
    matmuls = (1 if with_context else 0) + (5 if with_backward else 1)
    flops = 2 * tokens * keys * features * matmuls
    bytes_accessed = sum(a.size * a.dtype.itemsize for a in args) + sum(
        math.prod(o.shape) * o.dtype.itemsize for o in outs
    )
    vmem = pl.BlockSpec(memory_space=pltpu.VMEM)
    return pl.pallas_call(
        functools.partial(attention_kernel, scaling, with_context, with_backward),
        out_shape=outs,
        in_specs=[vmem] * len(args),
        out_specs=[vmem] * len(outs),
        cost_estimate=pl.CostEstimate(
            flops=flops, transcendentals=tokens * keys * HEADS, bytes_accessed=bytes_accessed
        ),
        compiler_params=pltpu.CompilerParams(vmem_limit_bytes=48 * 1024 * 1024),
    )(*args)


def body(queries_keys, values, cotangent):
    sizes = (lax.axis_size("lat"), lax.axis_size("lon"), lax.axis_size("pipe"))
    is_first = lax.axis_index("pipe") == 0
    tile_rows, tile_cols, features = cotangent.shape
    margin = MARGIN
    rows_ext = tile_rows + 2 * margin
    cols_ext = tile_cols + 2 * margin
    window_size = rows_ext * cols_ext
    keys = -(-window_size // 128) * 128
    token_count = tile_rows * tile_cols
    scaling = 1.0 / math.sqrt(features // HEADS)

    def flat_keys(window):
        flat = window.reshape(window_size, features)
        return jnp.concatenate([flat, jnp.zeros((keys - window_size, features), flat.dtype)], axis=0)

    def window_of(flat):
        return flat[:window_size].reshape(rows_ext, cols_ext, features)

    q = queries_keys[0, 0].reshape(token_count, features)
    lat_rows = lax.axis_index("lat") * tile_rows - margin + jnp.arange(rows_ext, dtype=jnp.int32)
    inside = (lat_rows >= 0) & (lat_rows < tile_rows * sizes[0])
    allowed = jnp.broadcast_to(inside[:, None], (rows_ext, cols_ext)).reshape(window_size)
    allowed = jnp.concatenate([allowed, jnp.zeros((keys - window_size,), bool)])
    mask = allowed.astype(jnp.float32)[None, :]

    kv = gather_window(jnp.stack([queries_keys[0, 1], values[0]], axis=2), sizes)
    k = flat_keys(kv[:, :, 0])
    v_win = kv[:, :, 1]

    (context_a,) = attention(mask, q, k, flat_keys(v_win), scaling=scaling)
    context_a = context_a.reshape(tile_rows, tile_cols, features)

    c_win = gather_window(context_a, sizes, src_pipe=0, dst_pipe=1)
    u_win = (v_win.astype(jnp.float32) + c_win.astype(jnp.float32)).astype(jnp.bfloat16)
    u = flat_keys(u_win)

    d_b = cotangent.reshape(token_count, features)
    context_b, gq_b, kterm_b, vterm_b = attention(mask, q, k, u, d_b, scaling=scaling)
    context_b = context_b.reshape(tile_rows, tile_cols, features)
    kterm_b = window_of(kterm_b)
    vterm_b = window_of(vterm_b)

    centre = slice(margin, margin + tile_rows), slice(margin, margin + tile_cols)
    got = scatter_pieces(vterm_b, sizes, src_pipe=1, dst_pipe=0)
    own_b = lax.ppermute(vterm_b[centre], AXES, pairs_from((0, 0), sizes, 1, 0))
    d_c = sum_pieces(own_b, got).astype(jnp.bfloat16).reshape(token_count, features)

    gq_c, kterm_c, vterm_c = attention(mask, q, k, u, d_c, with_context=False, scaling=scaling)
    kterm_c = window_of(kterm_c)
    vterm_c = window_of(vterm_c)

    terms = jnp.where(
        is_first, jnp.stack([kterm_c, vterm_c], axis=2), jnp.stack([kterm_b, vterm_b], axis=2)
    )
    back = scatter_pieces(terms, sizes)
    owned = sum_pieces(terms[centre], back).astype(jnp.bfloat16)

    activations = jnp.where(is_first, context_a, context_b)
    grad_q = jnp.where(is_first, gq_c, gq_b).reshape(tile_rows, tile_cols, features)
    grad_qk = jnp.stack([grad_q, owned[:, :, 0]], axis=0)
    return activations[None], grad_qk[None], owned[:, :, 1][None]


def solution(mesh):
    in_specs = (
        P("pipe", None, "lat", "lon", None),
        P("pipe", "lat", "lon", None),
        P("lat", "lon", None),
    )
    out_specs = (
        P("pipe", "lat", "lon", None),
        P("pipe", None, "lat", "lon", None),
        P("pipe", "lat", "lon", None),
    )
    return jax.shard_map(body, mesh=mesh, in_specs=in_specs, out_specs=out_specs, check_vma=False)
```

```python
import functools
import math

import jax
import jax.numpy as jnp
from jax import lax
from jax.experimental import pallas as pl
from jax.experimental.pallas import tpu as pltpu
from jax.sharding import PartitionSpec as P

HEADS = 12
MARGIN = 2

NEGATIVE = -1e30

AXES = ("lat", "lon", "pipe")


def linear(l, n, p, lons, pipes):
    return (l * lons + n) * pipes + p


def pairs_from(offset, sizes, src_pipe=None, dst_pipe=None):
    lats, lons, pipes = sizes
    dl, dn = offset
    out = []
    for l in range(lats):
        sl = l + dl
        if sl < 0 or sl >= lats:
            continue
        for n in range(lons):
            sn = (n + dn) % lons
            if src_pipe is None:
                for p in range(pipes):
                    out.append((linear(sl, sn, p, lons, pipes), linear(l, n, p, lons, pipes)))
            else:
                out.append((linear(sl, sn, src_pipe, lons, pipes), linear(l, n, dst_pipe, lons, pipes)))
    return out


def shifted(x, offset, sizes, src_pipe=None, dst_pipe=None):
    return lax.ppermute(x, AXES, pairs_from(offset, sizes, src_pipe, dst_pipe))


def flat(x):
    return x.reshape((-1,) + x.shape[2:])


def gather_keys(tile, sizes, src_pipe=None, dst_pipe=None):
    rows = tile.shape[0]
    if src_pipe is None:
        own = tile
    else:
        own = shifted(tile, (0, 0), sizes, src_pipe, dst_pipe)
    top = shifted(tile[rows - MARGIN :], (-1, 0), sizes, src_pipe, dst_pipe)
    bottom = shifted(tile[:MARGIN], (1, 0), sizes, src_pipe, dst_pipe)
    ext = jnp.concatenate([top, own, bottom], axis=0)
    cols = tile.shape[1]
    left = shifted(ext[:, cols - MARGIN :], (0, -1), sizes)
    right = shifted(ext[:, :MARGIN], (0, 1), sizes)
    return [flat(own), flat(top), flat(bottom), flat(left), flat(right)]


def piece_bounds(rows, cols):
    counts = [rows * cols, MARGIN * cols, MARGIN * cols, (rows + 2 * MARGIN) * MARGIN,
              (rows + 2 * MARGIN) * MARGIN]
    starts = [sum(counts[:i]) for i in range(len(counts))]
    return [(s, s + c) for s, c in zip(starts, counts)]


def place(piece, rows, cols, r0, c0):
    pad = [(r0, rows - r0 - piece.shape[0]), (c0, cols - c0 - piece.shape[1])]
    return jnp.pad(piece.astype(jnp.float32), pad + [(0, 0)] * (piece.ndim - 2))


def return_terms(terms, rows, cols, sizes, src_pipe=None, dst_pipe=None):
    tail = terms.shape[1:]
    (c0, c1), (t0, t1), (b0, b1), (l0, l1), (r0, r1) = piece_bounds(rows, cols)
    centre = terms[c0:c1].reshape((rows, cols) + tail)
    top = terms[t0:t1].astype(jnp.bfloat16)
    bottom = terms[b0:b1].astype(jnp.bfloat16)
    strip = (rows + 2 * MARGIN, MARGIN) + tail
    left = terms[l0:l1].astype(jnp.bfloat16).reshape(strip)
    right = terms[r0:r1].astype(jnp.bfloat16).reshape(strip)
    from_right = shifted(left, (0, 1), sizes)
    from_left = shifted(right, (0, -1), sizes)
    inner = slice(MARGIN, MARGIN + rows)
    partial = (
        centre
        + place(from_right[inner], rows, cols, 0, cols - MARGIN)
        + place(from_left[inner], rows, cols, 0, 0)
    )
    up = jnp.concatenate(
        [top, flat(from_left[:MARGIN]), flat(from_right[:MARGIN])], axis=0
    )
    down = jnp.concatenate(
        [bottom, flat(from_left[rows + MARGIN :]), flat(from_right[rows + MARGIN :])], axis=0
    )
    if src_pipe is not None:
        partial = shifted(partial, (0, 0), sizes, src_pipe, dst_pipe)
    from_below = shifted(up, (1, 0), sizes, src_pipe, dst_pipe)
    from_above = shifted(down, (-1, 0), sizes, src_pipe, dst_pipe)
    band = MARGIN * cols
    corner = MARGIN * MARGIN
    total = partial
    for got, r in ((from_above, 0), (from_below, rows - MARGIN)):
        total = total + place(got[:band].reshape((MARGIN, cols) + tail), rows, cols, r, 0)
        total = total + place(
            got[band : band + corner].reshape((MARGIN, MARGIN) + tail), rows, cols, r, 0
        )
        total = total + place(
            got[band + corner :].reshape((MARGIN, MARGIN) + tail), rows, cols, r, cols - MARGIN
        )
    return total


def attention_kernel(scaling, with_context, with_backward, *refs):
    mask_ref, q_ref, k_ref, u_ref = refs[:4]
    refs = refs[4:]
    if with_backward:
        d_ref, refs = refs[0], refs[1:]
    if with_context:
        c_ref, refs = refs[0], refs[1:]
    if with_backward:
        gq_ref, kt_ref, vt_ref = refs
    head_dim = q_ref.shape[1] // HEADS
    nt = (((1,), (1,)), ((), ()))

    def head(h, carry):
        lanes = pl.ds(pl.multiple_of(h * head_dim, head_dim), head_dim)
        qh = q_ref[:, lanes]
        kh = k_ref[:, lanes]
        uh = u_ref[:, lanes]
        scores = lax.dot_general(qh, kh, nt, preferred_element_type=jnp.float32) * scaling
        scores = jnp.where(mask_ref[...] > 0.5, scores, NEGATIVE)
        highest = jnp.max(scores, axis=1, keepdims=True)
        weights = jnp.exp(scores - highest)
        probs = weights / jnp.sum(weights, axis=1, keepdims=True)
        probs_low = probs.astype(jnp.bfloat16)
        if with_context:
            c_ref[:, lanes] = jnp.dot(
                probs_low, uh, preferred_element_type=jnp.float32
            ).astype(c_ref.dtype)
        if with_backward:
            dh = d_ref[:, lanes]
            dprob = lax.dot_general(dh, uh, nt, preferred_element_type=jnp.float32)
            inner = jnp.sum(probs * dprob, axis=1, keepdims=True)
            dscore = probs * (dprob - inner) * scaling
            gq_ref[:, lanes] = jnp.dot(
                dscore.astype(jnp.bfloat16), kh, preferred_element_type=jnp.float32
            ).astype(gq_ref.dtype)
            kt_ref[:, lanes] = jnp.dot(
                dscore.T.astype(jnp.bfloat16), qh, preferred_element_type=jnp.float32
            )
            vt_ref[:, lanes] = jnp.dot(
                probs.T.astype(jnp.bfloat16), dh, preferred_element_type=jnp.float32
            )
        return carry

    lax.fori_loop(0, HEADS, head, 0)


def attention(mask, q, k, u, d=None, with_context=True, scaling=1.0):
    tokens, features = q.shape
    keys = k.shape[0]
    with_backward = d is not None
    outs = []
    if with_context:
        outs.append(jax.ShapeDtypeStruct((tokens, features), jnp.bfloat16))
    if with_backward:
        outs += [
            jax.ShapeDtypeStruct((tokens, features), jnp.bfloat16),
            jax.ShapeDtypeStruct((keys, features), jnp.float32),
            jax.ShapeDtypeStruct((keys, features), jnp.float32),
        ]
    args = [mask, q, k, u] + ([d] if with_backward else [])
    matmuls = (1 if with_context else 0) + (5 if with_backward else 1)
    flops = 2 * tokens * keys * features * matmuls
    bytes_accessed = sum(a.size * a.dtype.itemsize for a in args) + sum(
        math.prod(o.shape) * o.dtype.itemsize for o in outs
    )
    vmem = pl.BlockSpec(memory_space=pltpu.VMEM)
    return pl.pallas_call(
        functools.partial(attention_kernel, scaling, with_context, with_backward),
        out_shape=outs,
        in_specs=[vmem] * len(args),
        out_specs=[vmem] * len(outs),
        cost_estimate=pl.CostEstimate(
            flops=flops, transcendentals=tokens * keys * HEADS, bytes_accessed=bytes_accessed
        ),
        compiler_params=pltpu.CompilerParams(vmem_limit_bytes=48 * 1024 * 1024),
    )(*args)


def body(queries_keys, values, cotangent):
    sizes = (lax.axis_size("lat"), lax.axis_size("lon"), lax.axis_size("pipe"))
    is_first = lax.axis_index("pipe") == 0
    tile_rows, tile_cols, features = cotangent.shape
    margin = MARGIN
    token_count = tile_rows * tile_cols
    bounds = piece_bounds(tile_rows, tile_cols)
    window_size = bounds[-1][1]
    keys = -(-window_size // 128) * 128
    scaling = 1.0 / math.sqrt(features // HEADS)

    def keys_of(pieces):
        pad = jnp.zeros((keys - window_size,) + pieces[0].shape[1:], pieces[0].dtype)
        return jnp.concatenate(pieces + [pad], axis=0)

    lat = lax.axis_index("lat")
    has_above = lat > 0
    has_below = lat < sizes[0] - 1
    strip_row = jnp.arange((tile_rows + 2 * margin) * margin, dtype=jnp.int32) // margin
    strip_ok = ((strip_row >= margin) | has_above) & ((strip_row < tile_rows + margin) | has_below)
    allowed = jnp.concatenate(
        [
            jnp.ones((token_count,), bool),
            jnp.broadcast_to(has_above, (margin * tile_cols,)),
            jnp.broadcast_to(has_below, (margin * tile_cols,)),
            strip_ok,
            strip_ok,
            jnp.zeros((keys - window_size,), bool),
        ]
    )
    mask = allowed.astype(jnp.float32)[None, :]

    q = queries_keys[0, 0].reshape(token_count, features)

    kv = keys_of(gather_keys(jnp.stack([queries_keys[0, 1], values[0]], axis=2), sizes))
    k = kv[:, 0]
    v = kv[:, 1]

    (context_a,) = attention(mask, q, k, v, scaling=scaling)

    c = keys_of(gather_keys(context_a.reshape(tile_rows, tile_cols, features), sizes, 0, 1))
    u = (v.astype(jnp.float32) + c.astype(jnp.float32)).astype(jnp.bfloat16)

    d_b = cotangent.reshape(token_count, features)
    context_b, gq_b, kterm_b, vterm_b = attention(mask, q, k, u, d_b, scaling=scaling)

    d_c = return_terms(vterm_b, tile_rows, tile_cols, sizes, 1, 0).astype(jnp.bfloat16)

    gq_c, kterm_c, vterm_c = attention(
        mask, q, k, u, d_c.reshape(token_count, features), with_context=False, scaling=scaling
    )

    terms = jnp.where(
        is_first, jnp.stack([kterm_c, vterm_c], axis=1), jnp.stack([kterm_b, vterm_b], axis=1)
    )
    owned = return_terms(terms, tile_rows, tile_cols, sizes).astype(jnp.bfloat16)

    activations = jnp.where(is_first, context_a, context_b).reshape(tile_rows, tile_cols, features)
    grad_q = jnp.where(is_first, gq_c, gq_b).reshape(tile_rows, tile_cols, features)
    grad_qk = jnp.stack([grad_q, owned[:, :, 0]], axis=0)
    return activations[None], grad_qk[None], owned[:, :, 1][None]


def solution(mesh):
    in_specs = (
        P("pipe", None, "lat", "lon", None),
        P("pipe", "lat", "lon", None),
        P("lat", "lon", None),
    )
    out_specs = (
        P("pipe", "lat", "lon", None),
        P("pipe", None, "lat", "lon", None),
        P("pipe", "lat", "lon", None),
    )
    return jax.shard_map(body, mesh=mesh, in_specs=in_specs, out_specs=out_specs, check_vma=False)
```

```python
import functools
import math

import jax
import jax.numpy as jnp
from jax import lax
from jax.experimental import pallas as pl
from jax.experimental.pallas import tpu as pltpu
from jax.sharding import PartitionSpec as P

HEADS = 12
MARGIN = 2

NEGATIVE = -1e30

AXES = ("lat", "lon", "pipe")


def linear(l, n, p, lons, pipes):
    return (l * lons + n) * pipes + p


def pairs_from(offset, sizes, src_pipe=None, dst_pipe=None):
    lats, lons, pipes = sizes
    dl, dn = offset
    out = []
    for l in range(lats):
        sl = l + dl
        if sl < 0 or sl >= lats:
            continue
        for n in range(lons):
            sn = (n + dn) % lons
            if src_pipe is None:
                for p in range(pipes):
                    out.append((linear(sl, sn, p, lons, pipes), linear(l, n, p, lons, pipes)))
            else:
                out.append((linear(sl, sn, src_pipe, lons, pipes), linear(l, n, dst_pipe, lons, pipes)))
    return out


def shifted(x, offset, sizes, src_pipe=None, dst_pipe=None):
    return lax.ppermute(x, AXES, pairs_from(offset, sizes, src_pipe, dst_pipe))


def flat(x):
    return x.reshape((-1,) + x.shape[2:])


def gather_keys(tile, sizes, src_pipe=None, dst_pipe=None):
    rows = tile.shape[0]
    if src_pipe is None:
        own = tile
    else:
        own = shifted(tile, (0, 0), sizes, src_pipe, dst_pipe)
    top = shifted(tile[rows - MARGIN :], (-1, 0), sizes, src_pipe, dst_pipe)
    bottom = shifted(tile[:MARGIN], (1, 0), sizes, src_pipe, dst_pipe)
    ext = jnp.concatenate([top, own, bottom], axis=0)
    cols = tile.shape[1]
    left = shifted(ext[:, cols - MARGIN :], (0, -1), sizes)
    right = shifted(ext[:, :MARGIN], (0, 1), sizes)
    return [flat(own), flat(top), flat(bottom), flat(left), flat(right)]


def piece_bounds(rows, cols):
    counts = [rows * cols, MARGIN * cols, MARGIN * cols, (rows + 2 * MARGIN) * MARGIN,
              (rows + 2 * MARGIN) * MARGIN]
    starts = [sum(counts[:i]) for i in range(len(counts))]
    return [(s, s + c) for s, c in zip(starts, counts)]


def place(piece, rows, cols, r0, c0):
    pad = [(r0, rows - r0 - piece.shape[0]), (c0, cols - c0 - piece.shape[1])]
    return jnp.pad(piece.astype(jnp.float32), pad + [(0, 0)] * (piece.ndim - 2))


def return_terms(terms, rows, cols, sizes, src_pipe=None, dst_pipe=None, centre=None):
    tail = terms.shape[1:]
    (c0, c1), (t0, t1), (b0, b1), (l0, l1), (r0, r1) = piece_bounds(rows, cols)
    if centre is None:
        centre = terms[c0:c1].reshape((rows, cols) + tail)
    top = terms[t0:t1].astype(jnp.bfloat16)
    bottom = terms[b0:b1].astype(jnp.bfloat16)
    strip = (rows + 2 * MARGIN, MARGIN) + tail
    left = terms[l0:l1].astype(jnp.bfloat16).reshape(strip)
    right = terms[r0:r1].astype(jnp.bfloat16).reshape(strip)
    from_right = shifted(left, (0, 1), sizes)
    from_left = shifted(right, (0, -1), sizes)
    inner = slice(MARGIN, MARGIN + rows)
    sides = jnp.stack([from_right[inner], from_left[inner]], axis=0)
    if src_pipe is not None:
        sides = shifted(sides, (0, 0), sizes, src_pipe, dst_pipe)
    partial = (
        centre
        + place(sides[0], rows, cols, 0, cols - MARGIN)
        + place(sides[1], rows, cols, 0, 0)
    )
    up = jnp.concatenate(
        [top, flat(from_left[:MARGIN]), flat(from_right[:MARGIN])], axis=0
    )
    down = jnp.concatenate(
        [bottom, flat(from_left[rows + MARGIN :]), flat(from_right[rows + MARGIN :])], axis=0
    )
    from_below = shifted(up, (1, 0), sizes, src_pipe, dst_pipe)
    from_above = shifted(down, (-1, 0), sizes, src_pipe, dst_pipe)
    band = MARGIN * cols
    corner = MARGIN * MARGIN
    total = partial
    for got, r in ((from_above, 0), (from_below, rows - MARGIN)):
        total = total + place(got[:band].reshape((MARGIN, cols) + tail), rows, cols, r, 0)
        total = total + place(
            got[band : band + corner].reshape((MARGIN, MARGIN) + tail), rows, cols, r, 0
        )
        total = total + place(
            got[band + corner :].reshape((MARGIN, MARGIN) + tail), rows, cols, r, cols - MARGIN
        )
    return total


def attention_kernel(scaling, with_context, with_backward, with_vterm, *refs):
    mask_ref, q_ref, k_ref = refs[:3]
    refs = refs[3:]
    if with_context or with_backward:
        u_ref, refs = refs[0], refs[1:]
    if with_backward or with_vterm:
        d_ref, refs = refs[0], refs[1:]
    if with_context:
        c_ref, refs = refs[0], refs[1:]
    if with_backward:
        gq_ref, kt_ref, refs = refs[0], refs[1], refs[2:]
    if with_backward or with_vterm:
        (vt_ref,) = refs
    head_dim = q_ref.shape[1] // HEADS
    nt = (((1,), (1,)), ((), ()))

    def head(h, carry):
        lanes = pl.ds(pl.multiple_of(h * head_dim, head_dim), head_dim)
        qh = q_ref[:, lanes]
        kh = k_ref[:, lanes]
        scores = lax.dot_general(qh, kh, nt, preferred_element_type=jnp.float32) * scaling
        scores = jnp.where(mask_ref[...] > 0.5, scores, NEGATIVE)
        highest = jnp.max(scores, axis=1, keepdims=True)
        weights = jnp.exp(scores - highest)
        probs = weights / jnp.sum(weights, axis=1, keepdims=True)
        if with_context:
            uh = u_ref[:, lanes]
            c_ref[:, lanes] = jnp.dot(
                probs.astype(jnp.bfloat16), uh, preferred_element_type=jnp.float32
            ).astype(c_ref.dtype)
        if with_backward:
            uh = u_ref[:, lanes]
            dh = d_ref[:, lanes]
            dprob = lax.dot_general(dh, uh, nt, preferred_element_type=jnp.float32)
            inner = jnp.sum(probs * dprob, axis=1, keepdims=True)
            dscore = probs * (dprob - inner) * scaling
            gq_ref[:, lanes] = jnp.dot(
                dscore.astype(jnp.bfloat16), kh, preferred_element_type=jnp.float32
            ).astype(gq_ref.dtype)
            kt_ref[:, lanes] = jnp.dot(
                dscore.T.astype(jnp.bfloat16), qh, preferred_element_type=jnp.float32
            )
        if with_backward or with_vterm:
            dh = d_ref[:, lanes]
            vt_ref[:, lanes] = jnp.dot(
                probs.T.astype(jnp.bfloat16), dh, preferred_element_type=jnp.float32
            )
        return carry

    lax.fori_loop(0, HEADS, head, 0, unroll=True)


def attention(mask, q, k, u=None, d=None, with_context=True, scaling=1.0):
    tokens, features = q.shape
    keys = k.shape[0]
    with_backward = d is not None and u is not None
    with_vterm = d is not None and u is None
    outs = []
    if with_context:
        outs.append(jax.ShapeDtypeStruct((tokens, features), jnp.bfloat16))
    if with_backward:
        outs += [
            jax.ShapeDtypeStruct((tokens, features), jnp.bfloat16),
            jax.ShapeDtypeStruct((keys, features), jnp.float32),
        ]
    if with_backward or with_vterm:
        outs.append(jax.ShapeDtypeStruct((keys, features), jnp.float32))
    args = [mask, q, k] + [a for a in (u, d) if a is not None]
    matmuls = 1 + (1 if with_context else 0) + (4 if with_backward else 0) + (1 if with_vterm else 0)
    flops = 2 * tokens * keys * features * matmuls
    bytes_accessed = sum(a.size * a.dtype.itemsize for a in args) + sum(
        math.prod(o.shape) * o.dtype.itemsize for o in outs
    )
    vmem = pl.BlockSpec(memory_space=pltpu.VMEM)
    return pl.pallas_call(
        functools.partial(attention_kernel, scaling, with_context, with_backward, with_vterm),
        out_shape=outs,
        in_specs=[vmem] * len(args),
        out_specs=[vmem] * len(outs),
        cost_estimate=pl.CostEstimate(
            flops=flops, transcendentals=tokens * keys * HEADS, bytes_accessed=bytes_accessed
        ),
        compiler_params=pltpu.CompilerParams(vmem_limit_bytes=48 * 1024 * 1024),
    )(*args)


def body(queries_keys, values, cotangent):
    sizes = (lax.axis_size("lat"), lax.axis_size("lon"), lax.axis_size("pipe"))
    is_first = lax.axis_index("pipe") == 0
    tile_rows, tile_cols, features = cotangent.shape
    margin = MARGIN
    token_count = tile_rows * tile_cols
    bounds = piece_bounds(tile_rows, tile_cols)
    window_size = bounds[-1][1]
    keys = -(-window_size // 128) * 128
    scaling = 1.0 / math.sqrt(features // HEADS)

    def keys_of(pieces):
        pad = jnp.zeros((keys - window_size,) + pieces[0].shape[1:], pieces[0].dtype)
        return jnp.concatenate(pieces + [pad], axis=0)

    lat = lax.axis_index("lat")
    has_above = lat > 0
    has_below = lat < sizes[0] - 1
    strip_row = jnp.arange((tile_rows + 2 * margin) * margin, dtype=jnp.int32) // margin
    strip_ok = ((strip_row >= margin) | has_above) & ((strip_row < tile_rows + margin) | has_below)
    allowed = jnp.concatenate(
        [
            jnp.ones((token_count,), bool),
            jnp.broadcast_to(has_above, (margin * tile_cols,)),
            jnp.broadcast_to(has_below, (margin * tile_cols,)),
            strip_ok,
            strip_ok,
            jnp.zeros((keys - window_size,), bool),
        ]
    )
    mask = allowed.astype(jnp.float32)[None, :]

    q = queries_keys[0, 0].reshape(token_count, features)

    kv = keys_of(gather_keys(jnp.stack([queries_keys[0, 1], values[0]], axis=2), sizes))
    k = kv[:, 0]
    v = kv[:, 1]

    qk_other = shifted(jnp.concatenate([q, k], axis=0), (0, 0), sizes, 1, 0)
    d_b = cotangent.reshape(token_count, features)

    (context_a,) = attention(mask, q, k, v, scaling=scaling)

    c = keys_of(gather_keys(context_a.reshape(tile_rows, tile_cols, features), sizes, 0, 1))
    u = (v.astype(jnp.float32) + c.astype(jnp.float32)).astype(jnp.bfloat16)

    context_b, gq_b, kterm_b, vterm_b = attention(mask, q, k, u, d_b, scaling=scaling)

    qk_other, vterm_b = lax.optimization_barrier((qk_other, vterm_b))
    (vterm_other,) = attention(
        mask, qk_other[:token_count], qk_other[token_count:], d=d_b, with_context=False,
        scaling=scaling,
    )
    centre_other = vterm_other[:token_count].reshape(tile_rows, tile_cols, features)

    d_c = return_terms(vterm_b, tile_rows, tile_cols, sizes, 1, 0, centre_other)
    d_c = d_c.astype(jnp.bfloat16)

    gq_c, kterm_c, vterm_c = attention(
        mask, q, k, u, d_c.reshape(token_count, features), with_context=False, scaling=scaling
    )

    terms = jnp.where(
        is_first, jnp.stack([kterm_c, vterm_c], axis=1), jnp.stack([kterm_b, vterm_b], axis=1)
    )
    owned = return_terms(terms, tile_rows, tile_cols, sizes).astype(jnp.bfloat16)

    activations = jnp.where(is_first, context_a, context_b).reshape(tile_rows, tile_cols, features)
    grad_q = jnp.where(is_first, gq_c, gq_b).reshape(tile_rows, tile_cols, features)
    grad_qk = jnp.stack([grad_q, owned[:, :, 0]], axis=0)
    return activations[None], grad_qk[None], owned[:, :, 1][None]


def solution(mesh):
    in_specs = (
        P("pipe", None, "lat", "lon", None),
        P("pipe", "lat", "lon", None),
        P("lat", "lon", None),
    )
    out_specs = (
        P("pipe", "lat", "lon", None),
        P("pipe", None, "lat", "lon", None),
        P("pipe", "lat", "lon", None),
    )
    return jax.shard_map(body, mesh=mesh, in_specs=in_specs, out_specs=out_specs, check_vma=False)
```

```python
import functools
import math

import jax
import jax.numpy as jnp
from jax import lax
from jax.experimental import pallas as pl
from jax.experimental.pallas import tpu as pltpu
from jax.sharding import PartitionSpec as P

HEADS = 12
MARGIN = 2

NEGATIVE = -1e30

AXES = ("lat", "lon", "pipe")


def linear(l, n, p, lons, pipes):
    return (l * lons + n) * pipes + p


def pairs_from(offset, sizes, src_pipe=None, dst_pipe=None):
    lats, lons, pipes = sizes
    dl, dn = offset
    out = []
    for l in range(lats):
        sl = l + dl
        if sl < 0 or sl >= lats:
            continue
        for n in range(lons):
            sn = (n + dn) % lons
            if src_pipe is None:
                for p in range(pipes):
                    out.append((linear(sl, sn, p, lons, pipes), linear(l, n, p, lons, pipes)))
            else:
                out.append((linear(sl, sn, src_pipe, lons, pipes), linear(l, n, dst_pipe, lons, pipes)))
    return out


def shifted(x, offset, sizes, src_pipe=None, dst_pipe=None):
    return lax.ppermute(x, AXES, pairs_from(offset, sizes, src_pipe, dst_pipe))


def flat(x):
    return x.reshape((-1,) + x.shape[2:])


def gather_keys(tile, sizes, src_pipe=None, dst_pipe=None):
    rows = tile.shape[0]
    if src_pipe is None:
        own = tile
    else:
        own = shifted(tile, (0, 0), sizes, src_pipe, dst_pipe)
    top = shifted(tile[rows - MARGIN :], (-1, 0), sizes, src_pipe, dst_pipe)
    bottom = shifted(tile[:MARGIN], (1, 0), sizes, src_pipe, dst_pipe)
    ext = jnp.concatenate([top, own, bottom], axis=0)
    cols = tile.shape[1]
    left = shifted(ext[:, cols - MARGIN :], (0, -1), sizes)
    right = shifted(ext[:, :MARGIN], (0, 1), sizes)
    return [flat(own), flat(top), flat(bottom), flat(left), flat(right)]


def piece_bounds(rows, cols):
    counts = [rows * cols, MARGIN * cols, MARGIN * cols, (rows + 2 * MARGIN) * MARGIN,
              (rows + 2 * MARGIN) * MARGIN]
    starts = [sum(counts[:i]) for i in range(len(counts))]
    return [(s, s + c) for s, c in zip(starts, counts)]


def place(piece, rows, cols, r0, c0):
    pad = [(r0, rows - r0 - piece.shape[0]), (c0, cols - c0 - piece.shape[1])]
    return jnp.pad(piece.astype(jnp.float32), pad + [(0, 0)] * (piece.ndim - 2))


def return_terms(terms, rows, cols, sizes, src_pipe=None, dst_pipe=None, centre=None):
    tail = terms.shape[1:]
    (c0, c1), (t0, t1), (b0, b1), (l0, l1), (r0, r1) = piece_bounds(rows, cols)
    if centre is None:
        centre = terms[c0:c1].reshape((rows, cols) + tail)
    top = terms[t0:t1].astype(jnp.bfloat16)
    bottom = terms[b0:b1].astype(jnp.bfloat16)
    strip = (rows + 2 * MARGIN, MARGIN) + tail
    left = terms[l0:l1].astype(jnp.bfloat16).reshape(strip)
    right = terms[r0:r1].astype(jnp.bfloat16).reshape(strip)
    from_right = shifted(left, (0, 1), sizes)
    from_left = shifted(right, (0, -1), sizes)
    inner = slice(MARGIN, MARGIN + rows)
    sides = jnp.stack([from_right[inner], from_left[inner]], axis=0)
    if src_pipe is not None:
        sides = shifted(sides, (0, 0), sizes, src_pipe, dst_pipe)
    partial = (
        centre
        + place(sides[0], rows, cols, 0, cols - MARGIN)
        + place(sides[1], rows, cols, 0, 0)
    )
    band_shape = (MARGIN, cols) + tail
    up = jnp.concatenate(
        [top.reshape(band_shape), from_left[:MARGIN], from_right[:MARGIN]], axis=1
    )
    down = jnp.concatenate(
        [bottom.reshape(band_shape), from_left[rows + MARGIN :], from_right[rows + MARGIN :]],
        axis=1,
    )
    from_below = shifted(up, (1, 0), sizes, src_pipe, dst_pipe)
    from_above = shifted(down, (-1, 0), sizes, src_pipe, dst_pipe)
    total = partial
    for got, r in ((from_above, 0), (from_below, rows - MARGIN)):
        total = total + place(got[:, :cols], rows, cols, r, 0)
        total = total + place(got[:, cols : cols + MARGIN], rows, cols, r, 0)
        total = total + place(got[:, cols + MARGIN :], rows, cols, r, cols - MARGIN)
    return total


def attention_kernel(scaling, with_context, with_backward, with_vterm, *refs):
    mask_ref, q_ref, k_ref = refs[:3]
    refs = refs[3:]
    if with_context or with_backward:
        u_ref, refs = refs[0], refs[1:]
    if with_backward or with_vterm:
        d_ref, refs = refs[0], refs[1:]
    if with_context:
        c_ref, refs = refs[0], refs[1:]
    if with_backward:
        gq_ref, kt_ref, refs = refs[0], refs[1], refs[2:]
    if with_backward or with_vterm:
        (vt_ref,) = refs
    head_dim = q_ref.shape[1] // HEADS
    nt = (((1,), (1,)), ((), ()))

    def head(h, carry):
        lanes = pl.ds(pl.multiple_of(h * head_dim, head_dim), head_dim)
        qh = q_ref[:, lanes]
        kh = k_ref[:, lanes]
        scores = lax.dot_general(qh, kh, nt, preferred_element_type=jnp.float32) * scaling
        scores = jnp.where(mask_ref[...] > 0.5, scores, NEGATIVE)
        highest = jnp.max(scores, axis=1, keepdims=True)
        weights = jnp.exp(scores - highest)
        probs = weights / jnp.sum(weights, axis=1, keepdims=True)
        if with_context:
            uh = u_ref[:, lanes]
            c_ref[:, lanes] = jnp.dot(
                probs.astype(jnp.bfloat16), uh, preferred_element_type=jnp.float32
            ).astype(c_ref.dtype)
        if with_backward:
            uh = u_ref[:, lanes]
            dh = d_ref[:, lanes]
            dprob = lax.dot_general(dh, uh, nt, preferred_element_type=jnp.float32)
            inner = jnp.sum(probs * dprob, axis=1, keepdims=True)
            dscore = probs * (dprob - inner) * scaling
            gq_ref[:, lanes] = jnp.dot(
                dscore.astype(jnp.bfloat16), kh, preferred_element_type=jnp.float32
            ).astype(gq_ref.dtype)
            kt_ref[:, lanes] = jnp.dot(
                dscore.T.astype(jnp.bfloat16), qh, preferred_element_type=jnp.float32
            )
        if with_backward or with_vterm:
            dh = d_ref[:, lanes]
            vt_ref[:, lanes] = jnp.dot(
                probs.T.astype(jnp.bfloat16), dh, preferred_element_type=jnp.float32
            )
        return carry

    lax.fori_loop(0, HEADS, head, 0, unroll=True)


def attention(mask, q, k, u=None, d=None, with_context=True, scaling=1.0):
    tokens, features = q.shape
    keys = k.shape[0]
    with_backward = d is not None and u is not None
    with_vterm = d is not None and u is None
    outs = []
    if with_context:
        outs.append(jax.ShapeDtypeStruct((tokens, features), jnp.bfloat16))
    if with_backward:
        outs += [
            jax.ShapeDtypeStruct((tokens, features), jnp.bfloat16),
            jax.ShapeDtypeStruct((keys, features), jnp.float32),
        ]
    if with_backward or with_vterm:
        outs.append(jax.ShapeDtypeStruct((keys, features), jnp.float32))
    args = [mask, q, k] + [a for a in (u, d) if a is not None]
    matmuls = 1 + (1 if with_context else 0) + (4 if with_backward else 0) + (1 if with_vterm else 0)
    flops = 2 * tokens * keys * features * matmuls
    bytes_accessed = sum(a.size * a.dtype.itemsize for a in args) + sum(
        math.prod(o.shape) * o.dtype.itemsize for o in outs
    )
    vmem = pl.BlockSpec(memory_space=pltpu.VMEM)
    return pl.pallas_call(
        functools.partial(attention_kernel, scaling, with_context, with_backward, with_vterm),
        out_shape=outs,
        in_specs=[vmem] * len(args),
        out_specs=[vmem] * len(outs),
        cost_estimate=pl.CostEstimate(
            flops=flops, transcendentals=tokens * keys * HEADS, bytes_accessed=bytes_accessed
        ),
        compiler_params=pltpu.CompilerParams(vmem_limit_bytes=48 * 1024 * 1024),
    )(*args)


def body(queries_keys, values, cotangent):
    sizes = (lax.axis_size("lat"), lax.axis_size("lon"), lax.axis_size("pipe"))
    is_first = lax.axis_index("pipe") == 0
    tile_rows, tile_cols, features = cotangent.shape
    margin = MARGIN
    token_count = tile_rows * tile_cols
    bounds = piece_bounds(tile_rows, tile_cols)
    window_size = bounds[-1][1]
    keys = -(-window_size // 128) * 128
    scaling = 1.0 / math.sqrt(features // HEADS)

    def keys_of(pieces):
        pad = jnp.zeros((keys - window_size,) + pieces[0].shape[1:], pieces[0].dtype)
        return jnp.concatenate(pieces + [pad], axis=0)

    lat = lax.axis_index("lat")
    has_above = lat > 0
    has_below = lat < sizes[0] - 1
    strip_row = jnp.arange((tile_rows + 2 * margin) * margin, dtype=jnp.int32) // margin
    strip_ok = ((strip_row >= margin) | has_above) & ((strip_row < tile_rows + margin) | has_below)
    allowed = jnp.concatenate(
        [
            jnp.ones((token_count,), bool),
            jnp.broadcast_to(has_above, (margin * tile_cols,)),
            jnp.broadcast_to(has_below, (margin * tile_cols,)),
            strip_ok,
            strip_ok,
            jnp.zeros((keys - window_size,), bool),
        ]
    )
    mask = allowed.astype(jnp.float32)[None, :]

    q = queries_keys[0, 0].reshape(token_count, features)

    kv = keys_of(gather_keys(jnp.stack([queries_keys[0, 1], values[0]], axis=2), sizes))
    k = kv[:, 0]
    v = kv[:, 1]

    qk_other = shifted(jnp.concatenate([q, k], axis=0), (0, 0), sizes, 1, 0)
    d_b = cotangent.reshape(token_count, features)

    (context_a,) = attention(mask, q, k, v, scaling=scaling)

    c = keys_of(gather_keys(context_a.reshape(tile_rows, tile_cols, features), sizes, 0, 1))
    u = (v.astype(jnp.float32) + c.astype(jnp.float32)).astype(jnp.bfloat16)

    context_b, gq_b, kterm_b, vterm_b = attention(mask, q, k, u, d_b, scaling=scaling)

    qk_other, vterm_b = lax.optimization_barrier((qk_other, vterm_b))
    (vterm_other,) = attention(
        mask, qk_other[:token_count], qk_other[token_count:], d=d_b, with_context=False,
        scaling=scaling,
    )
    centre_other = vterm_other[:token_count].reshape(tile_rows, tile_cols, features)

    d_c = return_terms(vterm_b, tile_rows, tile_cols, sizes, 1, 0, centre_other)
    d_c = d_c.astype(jnp.bfloat16)

    gq_c, kterm_c, vterm_c = attention(
        mask, q, k, u, d_c.reshape(token_count, features), with_context=False, scaling=scaling
    )

    terms = jnp.where(
        is_first, jnp.stack([kterm_c, vterm_c], axis=1), jnp.stack([kterm_b, vterm_b], axis=1)
    )
    owned = return_terms(terms, tile_rows, tile_cols, sizes).astype(jnp.bfloat16)

    activations = jnp.where(is_first, context_a, context_b).reshape(tile_rows, tile_cols, features)
    grad_q = jnp.where(is_first, gq_c, gq_b).reshape(tile_rows, tile_cols, features)
    grad_qk = jnp.stack([grad_q, owned[:, :, 0]], axis=0)
    return activations[None], grad_qk[None], owned[:, :, 1][None]


def solution(mesh):
    in_specs = (
        P("pipe", None, "lat", "lon", None),
        P("pipe", "lat", "lon", None),
        P("lat", "lon", None),
    )
    out_specs = (
        P("pipe", "lat", "lon", None),
        P("pipe", None, "lat", "lon", None),
        P("pipe", "lat", "lon", None),
    )
    return jax.shard_map(body, mesh=mesh, in_specs=in_specs, out_specs=out_specs, check_vma=False)
```

```python
import functools
import math

import jax
import jax.numpy as jnp
from jax import lax
from jax.experimental import pallas as pl
from jax.experimental.pallas import tpu as pltpu
from jax.sharding import PartitionSpec as P

HEADS = 12
MARGIN = 2

NEGATIVE = -1e30

AXES = ("lat", "lon", "pipe")


def linear(l, n, p, lons, pipes):
    return (l * lons + n) * pipes + p


def pairs_from(offset, sizes, src_pipe=None, dst_pipe=None):
    lats, lons, pipes = sizes
    dl, dn = offset
    out = []
    for l in range(lats):
        sl = l + dl
        if sl < 0 or sl >= lats:
            continue
        for n in range(lons):
            sn = (n + dn) % lons
            if src_pipe is None:
                for p in range(pipes):
                    out.append((linear(sl, sn, p, lons, pipes), linear(l, n, p, lons, pipes)))
            else:
                out.append((linear(sl, sn, src_pipe, lons, pipes), linear(l, n, dst_pipe, lons, pipes)))
    return out


def shifted(x, offset, sizes, src_pipe=None, dst_pipe=None):
    return lax.ppermute(x, AXES, pairs_from(offset, sizes, src_pipe, dst_pipe))


def flat(x):
    return x.reshape((-1,) + x.shape[2:])


def gather_keys(tile, sizes, src_pipe=None, dst_pipe=None):
    rows = tile.shape[0]
    if src_pipe is None:
        own = tile
    else:
        own = shifted(tile, (0, 0), sizes, src_pipe, dst_pipe)
    top = shifted(tile[rows - MARGIN :], (-1, 0), sizes, src_pipe, dst_pipe)
    bottom = shifted(tile[:MARGIN], (1, 0), sizes, src_pipe, dst_pipe)
    ext = jnp.concatenate([top, own, bottom], axis=0)
    cols = tile.shape[1]
    left = shifted(ext[:, cols - MARGIN :], (0, -1), sizes)
    right = shifted(ext[:, :MARGIN], (0, 1), sizes)
    return [flat(own), flat(top), flat(bottom), flat(left), flat(right)]


def piece_bounds(rows, cols):
    counts = [rows * cols, MARGIN * cols, MARGIN * cols, (rows + 2 * MARGIN) * MARGIN,
              (rows + 2 * MARGIN) * MARGIN]
    starts = [sum(counts[:i]) for i in range(len(counts))]
    return [(s, s + c) for s, c in zip(starts, counts)]


def place(piece, rows, cols, r0, c0):
    pad = [(0, 0), (r0, rows - r0 - piece.shape[1]), (c0, cols - c0 - piece.shape[2]), (0, 0)]
    return jnp.pad(piece.astype(jnp.float32), pad)


def return_terms(pieces, rows, cols, sizes, src_pipe=None, dst_pipe=None, centre=None):
    own, top, bottom, left, right = pieces
    lead, features = own.shape[0], own.shape[-1]
    if centre is None:
        centre = own.reshape(lead, rows, cols, features)
    from_right = shifted(left, (0, 1), sizes)
    from_left = shifted(right, (0, -1), sizes)
    strip = (lead, rows + 2 * MARGIN, MARGIN, features)
    from_right = from_right.reshape(strip)
    from_left = from_left.reshape(strip)
    inner = slice(MARGIN, MARGIN + rows)
    sides = jnp.stack([from_right[:, inner], from_left[:, inner]], axis=0)
    if src_pipe is not None:
        sides = shifted(sides, (0, 0), sizes, src_pipe, dst_pipe)
    partial = (
        centre
        + place(sides[0], rows, cols, 0, cols - MARGIN)
        + place(sides[1], rows, cols, 0, 0)
    )
    band = (lead, MARGIN, cols, features)
    up = jnp.concatenate(
        [top.reshape(band), from_left[:, :MARGIN], from_right[:, :MARGIN]], axis=2
    )
    down = jnp.concatenate(
        [bottom.reshape(band), from_left[:, rows + MARGIN :], from_right[:, rows + MARGIN :]],
        axis=2,
    )
    from_below = shifted(up, (1, 0), sizes, src_pipe, dst_pipe)
    from_above = shifted(down, (-1, 0), sizes, src_pipe, dst_pipe)
    total = partial
    for got, r in ((from_above, 0), (from_below, rows - MARGIN)):
        total = total + place(got[:, :, :cols], rows, cols, r, 0)
        total = total + place(got[:, :, cols : cols + MARGIN], rows, cols, r, 0)
        total = total + place(got[:, :, cols + MARGIN :], rows, cols, r, cols - MARGIN)
    return total


def attention_kernel(scaling, bounds, with_context, with_grads, with_vterm, centre_only, *refs):
    mask_ref, q_ref, k_ref = refs[:3]
    refs = refs[3:]
    if with_context or with_grads:
        u_ref, refs = refs[0], refs[1:]
    if with_grads or with_vterm:
        d_ref, refs = refs[0], refs[1:]
    if with_context:
        c_ref, refs = refs[0], refs[1:]
    if with_grads:
        gq_ref, refs = refs[0], refs[1:]
    term_refs = refs
    head_dim = q_ref.shape[1] // HEADS
    nt = (((1,), (1,)), ((), ()))

    def store_terms(res, which, lanes):
        if centre_only:
            (c0, c1) = bounds[0]
            term_refs[0][which, :, lanes] = res[c0:c1]
            return
        for index, ((s0, s1), ref) in enumerate(zip(bounds, term_refs)):
            part = res[s0:s1]
            ref[which, :, lanes] = part if index == 0 else part.astype(ref.dtype)

    def head(h, carry):
        lanes = pl.ds(pl.multiple_of(h * head_dim, head_dim), head_dim)
        qh = q_ref[:, lanes]
        kh = k_ref[:, lanes]
        scores = lax.dot_general(qh, kh, nt, preferred_element_type=jnp.float32) * scaling
        scores = jnp.where(mask_ref[...] > 0.5, scores, NEGATIVE)
        highest = jnp.max(scores, axis=1, keepdims=True)
        weights = jnp.exp(scores - highest)
        probs = weights / jnp.sum(weights, axis=1, keepdims=True)
        if with_context:
            uh = u_ref[:, lanes]
            c_ref[:, lanes] = jnp.dot(
                probs.astype(jnp.bfloat16), uh, preferred_element_type=jnp.float32
            ).astype(c_ref.dtype)
        if with_grads:
            uh = u_ref[:, lanes]
            dh = d_ref[:, lanes]
            dprob = lax.dot_general(dh, uh, nt, preferred_element_type=jnp.float32)
            inner = jnp.sum(probs * dprob, axis=1, keepdims=True)
            dscore = probs * (dprob - inner) * scaling
            gq_ref[:, lanes] = jnp.dot(
                dscore.astype(jnp.bfloat16), kh, preferred_element_type=jnp.float32
            ).astype(gq_ref.dtype)
            kterm = jnp.dot(dscore.T.astype(jnp.bfloat16), qh, preferred_element_type=jnp.float32)
            store_terms(kterm, 0, lanes)
        if with_grads or with_vterm:
            dh = d_ref[:, lanes]
            vterm = jnp.dot(probs.T.astype(jnp.bfloat16), dh, preferred_element_type=jnp.float32)
            store_terms(vterm, 1 if with_grads else 0, lanes)
        return carry

    lax.fori_loop(0, HEADS, head, 0, unroll=True)


def attention(
    mask, q, k, bounds, u=None, d=None, with_context=True, grads=True, centre_only=False,
    scaling=1.0,
):
    tokens, features = q.shape
    keys = k.shape[0]
    with_grads = grads and d is not None and u is not None
    with_vterm = d is not None and not with_grads
    outs = []
    if with_context:
        outs.append(jax.ShapeDtypeStruct((tokens, features), jnp.bfloat16))
    if with_grads:
        outs.append(jax.ShapeDtypeStruct((tokens, features), jnp.bfloat16))
    lead = 2 if with_grads else 1
    if with_grads or with_vterm:
        for index, (s0, s1) in enumerate(bounds[: 1 if centre_only else len(bounds)]):
            dtype = jnp.float32 if index == 0 else jnp.bfloat16
            outs.append(jax.ShapeDtypeStruct((lead, s1 - s0, features), dtype))
    args = [mask, q, k] + [a for a in (u, d) if a is not None]
    matmuls = 1 + (1 if with_context else 0) + (4 if with_grads else 0) + (1 if with_vterm else 0)
    flops = 2 * tokens * keys * features * matmuls
    bytes_accessed = sum(a.size * a.dtype.itemsize for a in args) + sum(
        math.prod(o.shape) * o.dtype.itemsize for o in outs
    )
    vmem = pl.BlockSpec(memory_space=pltpu.VMEM)
    return pl.pallas_call(
        functools.partial(
            attention_kernel, scaling, tuple(bounds), with_context, with_grads, with_vterm,
            centre_only,
        ),
        out_shape=outs,
        in_specs=[vmem] * len(args),
        out_specs=[vmem] * len(outs),
        cost_estimate=pl.CostEstimate(
            flops=flops, transcendentals=tokens * keys * HEADS, bytes_accessed=bytes_accessed
        ),
        compiler_params=pltpu.CompilerParams(vmem_limit_bytes=48 * 1024 * 1024),
    )(*args)


def body(queries_keys, values, cotangent):
    sizes = (lax.axis_size("lat"), lax.axis_size("lon"), lax.axis_size("pipe"))
    is_first = lax.axis_index("pipe") == 0
    tile_rows, tile_cols, features = cotangent.shape
    margin = MARGIN
    token_count = tile_rows * tile_cols
    bounds = piece_bounds(tile_rows, tile_cols)
    window_size = bounds[-1][1]
    keys = -(-window_size // 128) * 128
    scaling = 1.0 / math.sqrt(features // HEADS)

    def keys_of(pieces):
        pad = jnp.zeros((keys - window_size,) + pieces[0].shape[1:], pieces[0].dtype)
        return jnp.concatenate(pieces + [pad], axis=0)

    lat = lax.axis_index("lat")
    has_above = lat > 0
    has_below = lat < sizes[0] - 1
    strip_row = jnp.arange((tile_rows + 2 * margin) * margin, dtype=jnp.int32) // margin
    strip_ok = ((strip_row >= margin) | has_above) & ((strip_row < tile_rows + margin) | has_below)
    allowed = jnp.concatenate(
        [
            jnp.ones((token_count,), bool),
            jnp.broadcast_to(has_above, (margin * tile_cols,)),
            jnp.broadcast_to(has_below, (margin * tile_cols,)),
            strip_ok,
            strip_ok,
            jnp.zeros((keys - window_size,), bool),
        ]
    )
    mask = allowed.astype(jnp.float32)[None, :]

    q = queries_keys[0, 0].reshape(token_count, features)
    cot = cotangent.reshape(token_count, features)

    kv = keys_of(gather_keys(jnp.stack([queries_keys[0, 1], values[0]], axis=2), sizes))
    k = kv[:, 0]
    v = kv[:, 1]

    qk_other = shifted(jnp.concatenate([q, k], axis=0), (0, 0), sizes, 1, 0)

    (context_a,) = attention(mask, q, k, bounds, v, scaling=scaling)

    c = keys_of(gather_keys(context_a.reshape(tile_rows, tile_cols, features), sizes, 0, 1))
    u = (v.astype(jnp.float32) + c.astype(jnp.float32)).astype(jnp.bfloat16)

    context_b, *vterm_b = attention(mask, q, k, bounds, u, cot, grads=False, scaling=scaling)

    qk_other, vterm_b = lax.optimization_barrier((qk_other, vterm_b))
    (centre_other,) = attention(
        mask, qk_other[:token_count], qk_other[token_count:], bounds, d=cot,
        with_context=False, centre_only=True, scaling=scaling,
    )
    centre_other = centre_other.reshape(1, tile_rows, tile_cols, features)

    d_c = return_terms(vterm_b, tile_rows, tile_cols, sizes, 1, 0, centre_other)
    d_c = jnp.where(is_first, d_c[0].astype(jnp.bfloat16).reshape(token_count, features), cot)

    grad_q, *terms = attention(mask, q, k, bounds, u, d_c, with_context=False, scaling=scaling)

    owned = return_terms(terms, tile_rows, tile_cols, sizes).astype(jnp.bfloat16)

    activations = jnp.where(is_first, context_a, context_b).reshape(tile_rows, tile_cols, features)
    grad_qk = jnp.stack([grad_q.reshape(tile_rows, tile_cols, features), owned[0]], axis=0)
    return activations[None], grad_qk[None], owned[1][None]


def solution(mesh):
    in_specs = (
        P("pipe", None, "lat", "lon", None),
        P("pipe", "lat", "lon", None),
        P("lat", "lon", None),
    )
    out_specs = (
        P("pipe", "lat", "lon", None),
        P("pipe", None, "lat", "lon", None),
        P("pipe", "lat", "lon", None),
    )
    return jax.shard_map(body, mesh=mesh, in_specs=in_specs, out_specs=out_specs, check_vma=False)
```

```python
import functools
import math

import jax
import jax.numpy as jnp
from jax import lax
from jax.experimental import pallas as pl
from jax.experimental.pallas import tpu as pltpu
from jax.sharding import PartitionSpec as P

HEADS = 12
MARGIN = 2

NEGATIVE = -1e30

AXES = ("lat", "lon", "pipe")


def linear(l, n, p, lons, pipes):
    return (l * lons + n) * pipes + p


def pairs_from(offset, sizes, src_pipe=None, dst_pipe=None):
    lats, lons, pipes = sizes
    dl, dn = offset
    out = []
    for l in range(lats):
        sl = l + dl
        if sl < 0 or sl >= lats:
            continue
        for n in range(lons):
            sn = (n + dn) % lons
            if src_pipe is None:
                for p in range(pipes):
                    out.append((linear(sl, sn, p, lons, pipes), linear(l, n, p, lons, pipes)))
            else:
                out.append((linear(sl, sn, src_pipe, lons, pipes), linear(l, n, dst_pipe, lons, pipes)))
    return out


def shifted(x, offset, sizes, src_pipe=None, dst_pipe=None):
    return lax.ppermute(x, AXES, pairs_from(offset, sizes, src_pipe, dst_pipe))


def flat(x):
    return x.reshape((-1,) + x.shape[2:])


def gather_keys(tile, sizes, src_pipe=None, dst_pipe=None):
    rows = tile.shape[0]
    if src_pipe is None:
        own = tile
    else:
        own = shifted(tile, (0, 0), sizes, src_pipe, dst_pipe)
    top = shifted(tile[rows - MARGIN :], (-1, 0), sizes, src_pipe, dst_pipe)
    bottom = shifted(tile[:MARGIN], (1, 0), sizes, src_pipe, dst_pipe)
    ext = jnp.concatenate([top, own, bottom], axis=0)
    cols = tile.shape[1]
    left = shifted(ext[:, cols - MARGIN :], (0, -1), sizes)
    right = shifted(ext[:, :MARGIN], (0, 1), sizes)
    return [flat(own), flat(top), flat(bottom), flat(left), flat(right)]


def piece_bounds(rows, cols):
    counts = [rows * cols, MARGIN * cols, MARGIN * cols, (rows + 2 * MARGIN) * MARGIN,
              (rows + 2 * MARGIN) * MARGIN]
    starts = [sum(counts[:i]) for i in range(len(counts))]
    return [(s, s + c) for s, c in zip(starts, counts)]


def place(piece, rows, cols, r0, c0):
    pad = [(0, 0), (r0, rows - r0 - piece.shape[1]), (c0, cols - c0 - piece.shape[2]), (0, 0)]
    return jnp.pad(piece.astype(jnp.float32), pad)


def return_terms(pieces, rows, cols, sizes, src_pipe=None, dst_pipe=None, centre=None):
    own, top, bottom, left, right = pieces
    lead, features = own.shape[0], own.shape[-1]
    if centre is None:
        centre = own.reshape(lead, rows, cols, features)
    from_right = shifted(left, (0, 1), sizes)
    from_left = shifted(right, (0, -1), sizes)
    strip = (lead, rows + 2 * MARGIN, MARGIN, features)
    from_right = from_right.reshape(strip)
    from_left = from_left.reshape(strip)
    inner = slice(MARGIN, MARGIN + rows)
    sides = jnp.stack([from_right[:, inner], from_left[:, inner]], axis=0)
    if src_pipe is not None:
        sides = shifted(sides, (0, 0), sizes, src_pipe, dst_pipe)
    partial = (
        centre
        + place(sides[0], rows, cols, 0, cols - MARGIN)
        + place(sides[1], rows, cols, 0, 0)
    )
    band = (lead, MARGIN, cols, features)
    up = jnp.concatenate(
        [top.reshape(band), from_left[:, :MARGIN], from_right[:, :MARGIN]], axis=2
    )
    down = jnp.concatenate(
        [bottom.reshape(band), from_left[:, rows + MARGIN :], from_right[:, rows + MARGIN :]],
        axis=2,
    )
    from_below = shifted(up, (1, 0), sizes, src_pipe, dst_pipe)
    from_above = shifted(down, (-1, 0), sizes, src_pipe, dst_pipe)
    total = partial
    for got, r in ((from_above, 0), (from_below, rows - MARGIN)):
        total = total + place(got[:, :, :cols], rows, cols, r, 0)
        total = total + place(got[:, :, cols : cols + MARGIN], rows, cols, r, 0)
        total = total + place(got[:, :, cols + MARGIN :], rows, cols, r, cols - MARGIN)
    return total


def attention_kernel(scaling, bounds, with_context, with_grads, with_vterm, centre_only, *refs):
    if centre_only:
        mask_ref, qk_ref = refs[:2]
        tokens = qk_ref.shape[0] - mask_ref.shape[1]
        q_ref = qk_ref.at[:tokens]
        k_ref = qk_ref.at[tokens:]
        refs = refs[2:]
    else:
        mask_ref, q_ref, k_ref = refs[:3]
        refs = refs[3:]
    if with_context or with_grads:
        u_ref, refs = refs[0], refs[1:]
    if with_grads or with_vterm:
        d_ref, refs = refs[0], refs[1:]
    if with_context:
        c_ref, refs = refs[0], refs[1:]
    if with_grads:
        gq_ref, refs = refs[0], refs[1:]
    term_refs = refs
    head_dim = q_ref.shape[1] // HEADS
    nt = (((1,), (1,)), ((), ()))

    def store_terms(res, which, lanes):
        if centre_only:
            (c0, c1) = bounds[0]
            term_refs[0][which, :, lanes] = res[c0:c1]
            return
        for index, ((s0, s1), ref) in enumerate(zip(bounds, term_refs)):
            part = res[s0:s1]
            ref[which, :, lanes] = part if index == 0 else part.astype(ref.dtype)

    def head(h, carry):
        lanes = pl.ds(pl.multiple_of(h * head_dim, head_dim), head_dim)
        qh = q_ref[:, lanes]
        kh = k_ref[:, lanes]
        scores = lax.dot_general(qh, kh, nt, preferred_element_type=jnp.float32) * scaling
        scores = jnp.where(mask_ref[...] > 0.5, scores, NEGATIVE)
        highest = jnp.max(scores, axis=1, keepdims=True)
        weights = jnp.exp(scores - highest)
        probs = weights / jnp.sum(weights, axis=1, keepdims=True)
        if with_context:
            uh = u_ref[:, lanes]
            c_ref[:, lanes] = jnp.dot(
                probs.astype(jnp.bfloat16), uh, preferred_element_type=jnp.float32
            ).astype(c_ref.dtype)
        if with_grads:
            uh = u_ref[:, lanes]
            dh = d_ref[:, lanes]
            dprob = lax.dot_general(dh, uh, nt, preferred_element_type=jnp.float32)
            inner = jnp.sum(probs * dprob, axis=1, keepdims=True)
            dscore = probs * (dprob - inner) * scaling
            gq_ref[:, lanes] = jnp.dot(
                dscore.astype(jnp.bfloat16), kh, preferred_element_type=jnp.float32
            ).astype(gq_ref.dtype)
            kterm = jnp.dot(dscore.T.astype(jnp.bfloat16), qh, preferred_element_type=jnp.float32)
            store_terms(kterm, 0, lanes)
        if with_grads or with_vterm:
            dh = d_ref[:, lanes]
            vterm = jnp.dot(probs.T.astype(jnp.bfloat16), dh, preferred_element_type=jnp.float32)
            store_terms(vterm, 1 if with_grads else 0, lanes)
        return carry

    lax.fori_loop(0, HEADS, head, 0, unroll=True)


def attention(
    mask, q, k, bounds, u=None, d=None, with_context=True, grads=True, centre_only=False,
    scaling=1.0,
):
    if centre_only:
        keys = mask.shape[1]
        tokens, features = q.shape[0] - keys, q.shape[1]
    else:
        tokens, features = q.shape
        keys = k.shape[0]
    with_grads = grads and d is not None and u is not None
    with_vterm = d is not None and not with_grads
    outs = []
    if with_context:
        outs.append(jax.ShapeDtypeStruct((tokens, features), jnp.bfloat16))
    if with_grads:
        outs.append(jax.ShapeDtypeStruct((tokens, features), jnp.bfloat16))
    lead = 2 if with_grads else 1
    if with_grads or with_vterm:
        for index, (s0, s1) in enumerate(bounds[: 1 if centre_only else len(bounds)]):
            dtype = jnp.float32 if index == 0 else jnp.bfloat16
            outs.append(jax.ShapeDtypeStruct((lead, s1 - s0, features), dtype))
    args = [mask, q] + ([] if centre_only else [k]) + [a for a in (u, d) if a is not None]
    matmuls = 1 + (1 if with_context else 0) + (4 if with_grads else 0) + (1 if with_vterm else 0)
    flops = 2 * tokens * keys * features * matmuls
    bytes_accessed = sum(a.size * a.dtype.itemsize for a in args) + sum(
        math.prod(o.shape) * o.dtype.itemsize for o in outs
    )
    vmem = pl.BlockSpec(memory_space=pltpu.VMEM)
    return pl.pallas_call(
        functools.partial(
            attention_kernel, scaling, tuple(bounds), with_context, with_grads, with_vterm,
            centre_only,
        ),
        out_shape=outs,
        in_specs=[vmem] * len(args),
        out_specs=[vmem] * len(outs),
        cost_estimate=pl.CostEstimate(
            flops=flops, transcendentals=tokens * keys * HEADS, bytes_accessed=bytes_accessed
        ),
        compiler_params=pltpu.CompilerParams(vmem_limit_bytes=48 * 1024 * 1024),
    )(*args)


def body(queries_keys, values, cotangent):
    sizes = (lax.axis_size("lat"), lax.axis_size("lon"), lax.axis_size("pipe"))
    is_first = lax.axis_index("pipe") == 0
    tile_rows, tile_cols, features = cotangent.shape
    margin = MARGIN
    token_count = tile_rows * tile_cols
    bounds = piece_bounds(tile_rows, tile_cols)
    window_size = bounds[-1][1]
    keys = -(-window_size // 128) * 128
    scaling = 1.0 / math.sqrt(features // HEADS)

    def keys_of(pieces):
        pad = jnp.zeros((keys - window_size,) + pieces[0].shape[1:], pieces[0].dtype)
        return jnp.concatenate(pieces + [pad], axis=0)

    lat = lax.axis_index("lat")
    has_above = lat > 0
    has_below = lat < sizes[0] - 1
    strip_row = jnp.arange((tile_rows + 2 * margin) * margin, dtype=jnp.int32) // margin
    strip_ok = ((strip_row >= margin) | has_above) & ((strip_row < tile_rows + margin) | has_below)
    allowed = jnp.concatenate(
        [
            jnp.ones((token_count,), bool),
            jnp.broadcast_to(has_above, (margin * tile_cols,)),
            jnp.broadcast_to(has_below, (margin * tile_cols,)),
            strip_ok,
            strip_ok,
            jnp.zeros((keys - window_size,), bool),
        ]
    )
    mask = allowed.astype(jnp.float32)[None, :]

    q = queries_keys[0, 0].reshape(token_count, features)
    cot = cotangent.reshape(token_count, features)

    kv = keys_of(gather_keys(jnp.stack([queries_keys[0, 1], values[0]], axis=2), sizes))
    k = kv[:, 0]
    v = kv[:, 1]

    qk_other = shifted(jnp.concatenate([q, k], axis=0), (0, 0), sizes, 1, 0)

    (context_a,) = attention(mask, q, k, bounds, v, scaling=scaling)

    c = keys_of(gather_keys(context_a.reshape(tile_rows, tile_cols, features), sizes, 0, 1))
    u = (v.astype(jnp.float32) + c.astype(jnp.float32)).astype(jnp.bfloat16)

    context_b, *vterm_b = attention(mask, q, k, bounds, u, cot, grads=False, scaling=scaling)

    qk_other, vterm_b = lax.optimization_barrier((qk_other, vterm_b))
    (centre_other,) = attention(
        mask, qk_other, None, bounds, d=cot, with_context=False, centre_only=True, scaling=scaling
    )
    centre_other = centre_other.reshape(1, tile_rows, tile_cols, features)

    d_c = return_terms(vterm_b, tile_rows, tile_cols, sizes, 1, 0, centre_other)
    d_c = jnp.where(is_first, d_c[0].astype(jnp.bfloat16).reshape(token_count, features), cot)

    grad_q, *terms = attention(mask, q, k, bounds, u, d_c, with_context=False, scaling=scaling)

    owned = return_terms(terms, tile_rows, tile_cols, sizes).astype(jnp.bfloat16)

    activations = jnp.where(is_first, context_a, context_b).reshape(tile_rows, tile_cols, features)
    grad_qk = jnp.stack([grad_q.reshape(tile_rows, tile_cols, features), owned[0]], axis=0)
    return activations[None], grad_qk[None], owned[1][None]


def solution(mesh):
    in_specs = (
        P("pipe", None, "lat", "lon", None),
        P("pipe", "lat", "lon", None),
        P("lat", "lon", None),
    )
    out_specs = (
        P("pipe", "lat", "lon", None),
        P("pipe", None, "lat", "lon", None),
        P("pipe", "lat", "lon", None),
    )
    return jax.shard_map(body, mesh=mesh, in_specs=in_specs, out_specs=out_specs, check_vma=False)
```

```python
import functools
import math

import jax
import jax.numpy as jnp
from jax import lax
from jax.experimental import pallas as pl
from jax.experimental.pallas import tpu as pltpu
from jax.sharding import PartitionSpec as P

HEADS = 12
MARGIN = 2

NEGATIVE = -1e30

AXES = ("lat", "lon", "pipe")


def linear(l, n, p, lons, pipes):
    return (l * lons + n) * pipes + p


def pairs_from(offset, sizes, src_pipe=None, dst_pipe=None):
    lats, lons, pipes = sizes
    dl, dn = offset
    out = []
    for l in range(lats):
        sl = l + dl
        if sl < 0 or sl >= lats:
            continue
        for n in range(lons):
            sn = (n + dn) % lons
            if src_pipe is None:
                for p in range(pipes):
                    out.append((linear(sl, sn, p, lons, pipes), linear(l, n, p, lons, pipes)))
            else:
                out.append((linear(sl, sn, src_pipe, lons, pipes), linear(l, n, dst_pipe, lons, pipes)))
    return out


def shifted(x, offset, sizes, src_pipe=None, dst_pipe=None):
    return lax.ppermute(x, AXES, pairs_from(offset, sizes, src_pipe, dst_pipe))


def flat(x):
    return x.reshape((-1,) + x.shape[2:])


def gather_keys(tile, sizes, src_pipe=None, dst_pipe=None):
    rows = tile.shape[0]
    if src_pipe is None:
        own = tile
    else:
        own = shifted(tile, (0, 0), sizes, src_pipe, dst_pipe)
    top = shifted(tile[rows - MARGIN :], (-1, 0), sizes, src_pipe, dst_pipe)
    bottom = shifted(tile[:MARGIN], (1, 0), sizes, src_pipe, dst_pipe)
    ext = jnp.concatenate([top, own, bottom], axis=0)
    cols = tile.shape[1]
    left = shifted(ext[:, cols - MARGIN :], (0, -1), sizes)
    right = shifted(ext[:, :MARGIN], (0, 1), sizes)
    return [flat(own), flat(top), flat(bottom), flat(left), flat(right)]


def piece_bounds(rows, cols):
    counts = [rows * cols, MARGIN * cols, MARGIN * cols, (rows + 2 * MARGIN) * MARGIN,
              (rows + 2 * MARGIN) * MARGIN]
    starts = [sum(counts[:i]) for i in range(len(counts))]
    return [(s, s + c) for s, c in zip(starts, counts)]


def place(piece, rows, cols, r0, c0):
    pad = [(0, 0), (r0, rows - r0 - piece.shape[1]), (c0, cols - c0 - piece.shape[2]), (0, 0)]
    return jnp.pad(piece.astype(jnp.float32), pad)


def return_terms(pieces, rows, cols, sizes, src_pipe=None, dst_pipe=None, centre=None):
    own, top, bottom, left, right = pieces
    lead, features = own.shape[0], own.shape[-1]
    if centre is None:
        centre = own.reshape(lead, rows, cols, features)
    from_right = shifted(left, (0, 1), sizes)
    from_left = shifted(right, (0, -1), sizes)
    strip = (lead, rows + 2 * MARGIN, MARGIN, features)
    from_right = from_right.reshape(strip)
    from_left = from_left.reshape(strip)
    inner = slice(MARGIN, MARGIN + rows)
    sides = jnp.stack([from_right[:, inner], from_left[:, inner]], axis=0)
    if src_pipe is not None:
        sides = shifted(sides, (0, 0), sizes, src_pipe, dst_pipe)
    partial = (
        centre
        + place(sides[0], rows, cols, 0, cols - MARGIN)
        + place(sides[1], rows, cols, 0, 0)
    )
    band = (lead, MARGIN, cols, features)
    up = jnp.concatenate(
        [top.reshape(band), from_left[:, :MARGIN], from_right[:, :MARGIN]], axis=2
    )
    down = jnp.concatenate(
        [bottom.reshape(band), from_left[:, rows + MARGIN :], from_right[:, rows + MARGIN :]],
        axis=2,
    )
    from_below = shifted(up, (1, 0), sizes, src_pipe, dst_pipe)
    from_above = shifted(down, (-1, 0), sizes, src_pipe, dst_pipe)
    total = partial
    for got, r in ((from_above, 0), (from_below, rows - MARGIN)):
        total = total + place(got[:, :, :cols], rows, cols, r, 0)
        total = total + place(got[:, :, cols : cols + MARGIN], rows, cols, r, 0)
        total = total + place(got[:, :, cols + MARGIN :], rows, cols, r, cols - MARGIN)
    return total


def attention_kernel(scaling, bounds, with_context, with_grads, with_vterm, centre_only, *refs):
    if centre_only:
        mask_ref, qk_ref = refs[:2]
        tokens = qk_ref.shape[0] - mask_ref.shape[1]
        q_ref = qk_ref.at[:tokens]
        k_ref = qk_ref.at[tokens:]
        refs = refs[2:]
    else:
        mask_ref, q_ref, k_ref = refs[:3]
        refs = refs[3:]
    if with_context or with_grads:
        u_ref, refs = refs[0], refs[1:]
    if with_grads or with_vterm:
        d_ref, refs = refs[0], refs[1:]
    if with_context:
        c_ref, refs = refs[0], refs[1:]
    if with_grads:
        gq_ref, refs = refs[0], refs[1:]
    term_refs = refs
    head_dim = q_ref.shape[1] // HEADS
    nt = (((1,), (1,)), ((), ()))
    tn = (((0,), (0,)), ((), ()))

    def store_terms(res, which, lanes):
        if centre_only:
            (c0, c1) = bounds[0]
            term_refs[0][which, :, lanes] = res[c0:c1]
            return
        for index, ((s0, s1), ref) in enumerate(zip(bounds, term_refs)):
            part = res[s0:s1]
            ref[which, :, lanes] = part if index == 0 else part.astype(ref.dtype)

    def head(h, carry):
        lanes = pl.ds(pl.multiple_of(h * head_dim, head_dim), head_dim)
        qh = q_ref[:, lanes]
        kh = k_ref[:, lanes]
        scores = lax.dot_general(qh, kh, nt, preferred_element_type=jnp.float32) * scaling
        scores = jnp.where(mask_ref[...] > 0.5, scores, NEGATIVE)
        highest = jnp.max(scores, axis=1, keepdims=True)
        weights = jnp.exp(scores - highest)
        probs = weights / jnp.sum(weights, axis=1, keepdims=True)
        if with_context:
            uh = u_ref[:, lanes]
            c_ref[:, lanes] = jnp.dot(
                probs.astype(jnp.bfloat16), uh, preferred_element_type=jnp.float32
            ).astype(c_ref.dtype)
        if with_grads:
            uh = u_ref[:, lanes]
            dh = d_ref[:, lanes]
            dprob = lax.dot_general(dh, uh, nt, preferred_element_type=jnp.float32)
            inner = jnp.sum(probs * dprob, axis=1, keepdims=True)
            dscore = probs * (dprob - inner) * scaling
            gq_ref[:, lanes] = jnp.dot(
                dscore.astype(jnp.bfloat16), kh, preferred_element_type=jnp.float32
            ).astype(gq_ref.dtype)
            kterm = lax.dot_general(
                dscore.astype(jnp.bfloat16), qh, tn, preferred_element_type=jnp.float32
            )
            store_terms(kterm, 0, lanes)
        if with_grads or with_vterm:
            dh = d_ref[:, lanes]
            vterm = lax.dot_general(
                probs.astype(jnp.bfloat16), dh, tn, preferred_element_type=jnp.float32
            )
            store_terms(vterm, 1 if with_grads else 0, lanes)
        return carry

    lax.fori_loop(0, HEADS, head, 0, unroll=True)


def attention(
    mask, q, k, bounds, u=None, d=None, with_context=True, grads=True, centre_only=False,
    scaling=1.0,
):
    if centre_only:
        keys = mask.shape[1]
        tokens, features = q.shape[0] - keys, q.shape[1]
    else:
        tokens, features = q.shape
        keys = k.shape[0]
    with_grads = grads and d is not None and u is not None
    with_vterm = d is not None and not with_grads
    outs = []
    if with_context:
        outs.append(jax.ShapeDtypeStruct((tokens, features), jnp.bfloat16))
    if with_grads:
        outs.append(jax.ShapeDtypeStruct((tokens, features), jnp.bfloat16))
    lead = 2 if with_grads else 1
    if with_grads or with_vterm:
        for index, (s0, s1) in enumerate(bounds[: 1 if centre_only else len(bounds)]):
            dtype = jnp.float32 if index == 0 else jnp.bfloat16
            outs.append(jax.ShapeDtypeStruct((lead, s1 - s0, features), dtype))
    args = [mask, q] + ([] if centre_only else [k]) + [a for a in (u, d) if a is not None]
    matmuls = 1 + (1 if with_context else 0) + (4 if with_grads else 0) + (1 if with_vterm else 0)
    flops = 2 * tokens * keys * features * matmuls
    bytes_accessed = sum(a.size * a.dtype.itemsize for a in args) + sum(
        math.prod(o.shape) * o.dtype.itemsize for o in outs
    )
    vmem = pl.BlockSpec(memory_space=pltpu.VMEM)
    return pl.pallas_call(
        functools.partial(
            attention_kernel, scaling, tuple(bounds), with_context, with_grads, with_vterm,
            centre_only,
        ),
        out_shape=outs,
        in_specs=[vmem] * len(args),
        out_specs=[vmem] * len(outs),
        cost_estimate=pl.CostEstimate(
            flops=flops, transcendentals=tokens * keys * HEADS, bytes_accessed=bytes_accessed
        ),
        compiler_params=pltpu.CompilerParams(vmem_limit_bytes=48 * 1024 * 1024),
    )(*args)


def body(queries_keys, values, cotangent):
    sizes = (lax.axis_size("lat"), lax.axis_size("lon"), lax.axis_size("pipe"))
    is_first = lax.axis_index("pipe") == 0
    tile_rows, tile_cols, features = cotangent.shape
    margin = MARGIN
    token_count = tile_rows * tile_cols
    bounds = piece_bounds(tile_rows, tile_cols)
    window_size = bounds[-1][1]
    keys = -(-window_size // 128) * 128
    scaling = 1.0 / math.sqrt(features // HEADS)

    def keys_of(pieces):
        pad = jnp.zeros((keys - window_size,) + pieces[0].shape[1:], pieces[0].dtype)
        return jnp.concatenate(pieces + [pad], axis=0)

    lat = lax.axis_index("lat")
    has_above = lat > 0
    has_below = lat < sizes[0] - 1
    strip_row = jnp.arange((tile_rows + 2 * margin) * margin, dtype=jnp.int32) // margin
    strip_ok = ((strip_row >= margin) | has_above) & ((strip_row < tile_rows + margin) | has_below)
    allowed = jnp.concatenate(
        [
            jnp.ones((token_count,), bool),
            jnp.broadcast_to(has_above, (margin * tile_cols,)),
            jnp.broadcast_to(has_below, (margin * tile_cols,)),
            strip_ok,
            strip_ok,
            jnp.zeros((keys - window_size,), bool),
        ]
    )
    mask = allowed.astype(jnp.float32)[None, :]

    q = queries_keys[0, 0].reshape(token_count, features)
    cot = cotangent.reshape(token_count, features)

    kv = keys_of(gather_keys(jnp.stack([queries_keys[0, 1], values[0]], axis=2), sizes))
    k = kv[:, 0]
    v = kv[:, 1]

    qk_other = shifted(jnp.concatenate([q, k], axis=0), (0, 0), sizes, 1, 0)

    (context_a,) = attention(mask, q, k, bounds, v, scaling=scaling)

    c = keys_of(gather_keys(context_a.reshape(tile_rows, tile_cols, features), sizes, 0, 1))
    u = (v.astype(jnp.float32) + c.astype(jnp.float32)).astype(jnp.bfloat16)

    context_b, *vterm_b = attention(mask, q, k, bounds, u, cot, grads=False, scaling=scaling)

    qk_other, vterm_b = lax.optimization_barrier((qk_other, vterm_b))
    (centre_other,) = attention(
        mask, qk_other, None, bounds, d=cot, with_context=False, centre_only=True, scaling=scaling
    )
    centre_other = centre_other.reshape(1, tile_rows, tile_cols, features)

    d_c = return_terms(vterm_b, tile_rows, tile_cols, sizes, 1, 0, centre_other)
    d_c = jnp.where(is_first, d_c[0].astype(jnp.bfloat16).reshape(token_count, features), cot)

    grad_q, *terms = attention(mask, q, k, bounds, u, d_c, with_context=False, scaling=scaling)

    owned = return_terms(terms, tile_rows, tile_cols, sizes).astype(jnp.bfloat16)

    activations = jnp.where(is_first, context_a, context_b).reshape(tile_rows, tile_cols, features)
    grad_qk = jnp.stack([grad_q.reshape(tile_rows, tile_cols, features), owned[0]], axis=0)
    return activations[None], grad_qk[None], owned[1][None]


def solution(mesh):
    in_specs = (
        P("pipe", None, "lat", "lon", None),
        P("pipe", "lat", "lon", None),
        P("lat", "lon", None),
    )
    out_specs = (
        P("pipe", "lat", "lon", None),
        P("pipe", None, "lat", "lon", None),
        P("pipe", "lat", "lon", None),
    )
    return jax.shard_map(body, mesh=mesh, in_specs=in_specs, out_specs=out_specs, check_vma=False)
```
